32 devices in a mesh: vis: 8 (over y, x, core), tile: 4 (over z).
Axes of the slice: x: 2, y: 2, z: 4, core: 2. Of those that a mesh axis runs over, the one named last changes fastest.
Arguments:
- image: float32 [8192, 8192], P('vis', 'tile'), may hold values from 0 to 2
- extrapolated: float32 [8192, 8192], P('vis', 'tile'), may hold values from -6 to 6
- vis_dual: float32 [8192, 2, 128], P(('vis', 'tile')), may hold values from -6 to 6
- tree_dual: float32 [2, 8192, 4096], P(None, 'vis', 'tile'), may hold values from -6 to 6
- observed: float32 [8192, 2, 128], P(('vis', 'tile')), may hold values from -6 to 6
- kernel: float32 [128, 128], replicated, may hold values from -0.5 to 0.5
- block_index: int32 [8192], P(('vis', 'tile')), may hold values from 0 to 16383
- live_blocks: int32 [32], P(('vis', 'tile')), may hold values from 1 to 256, as said below
Outputs:
- image_next: float32 [8192, 8192], P('vis', 'tile')
- vis_next: float32 [8192, 2, 128], P(('vis', 'tile'))
- tree_next: float32 [2, 8192, 4096], P(None, 'vis', 'tile')
The draws below stay inside these ranges and needn't reach their ends.
Inputs may be any that keep to these rules, and one draw needn't show every extreme that they name: Each device's live slots are its first live_blocks entries of 256; some device has all 256 live in every draw.
All inputs are finite; a program needn't handle non-finite values.
Results may differ from the reference program's by a relative error of at most 0.00005.
Values sent between devices are 32-bit elements; how exact they have to be, the bound alone decides.
No kernel may reach another device: no remote copies, remote signals or barrier semaphores. Data moves between devices by JAX's collectives and lax.ppermute only.
A program may use at most 192 MiB of HBM per device.

```python
import jax
import jax.numpy as jnp
from jax import lax

NX = 8192
NYW = 8192
BW = 128
CAP = 256
FACET = 1024
ROWS = 2048
UVB = 16384
VBLOCKS = 8192
N_VIS = 8
N_TILE = 4


def draw_live_blocks(key, part):
    device_ids = jnp.arange(N_VIS * N_TILE, dtype=jnp.int32)
    lowest = CAP // 3
    rising = lowest + (CAP - lowest) * device_ids // max(N_VIS * N_TILE - 1, 1)
    jitter = jax.random.randint(key, (N_VIS * N_TILE,), -(CAP // 8), CAP // 8 + 1)
    counts = jnp.clip(rising + jitter, 1, CAP)
    chosen = jax.random.randint(jax.random.fold_in(key, 7), (), 0, N_VIS * N_TILE)
    return jnp.where(device_ids == chosen, CAP, counts).astype(jnp.int32)


def touch_ends(array, stream_key, smallest, high):
    longest = array.shape.index(max(array.shape))
    spots = []
    for shift in (0, 1):
        where = [jax.random.randint(jax.random.fold_in(stream_key, axis), (), 0, length) for axis, length in enumerate(array.shape)]
        where[longest] = (where[longest] + shift) % array.shape[longest]
        spots.append(tuple(where))
    return array.at[spots[0]].set(smallest).at[spots[1]].set(high)


def shard_levels(own_key, shape, cuts, smallest, top_value):
    factor_of = 1.0
    for dim, parts in cuts:
        heights = jax.random.uniform(jax.random.fold_in(jax.random.fold_in(own_key, 6), dim), (parts,), jnp.float32, smallest / len(cuts), top_value / len(cuts))
        factor_of = factor_of * jnp.repeat(jnp.exp(heights), shape[dim] // parts).reshape((-1,) + (1,) * (len(shape) - 1 - dim))
    return factor_of


def centred(stream_key, dims, spread, bound, shards=(), held_as=jnp.bfloat16):
    drawn = spread * jax.random.normal(stream_key, dims, jnp.float32)
    if shards:
        drawn = drawn * shard_levels(stream_key, dims, shards, -0.22, 0.18)
    return jnp.clip(drawn, -bound, bound).astype(held_as)


def setup_inputs(seed: int = 0) -> dict:
    keys = jax.random.split(jax.random.key(seed), 9)
    return {
        "image": jnp.clip(2.0 * jax.random.uniform(keys[0], (NX, NYW), jnp.float32) ** shard_levels(keys[0], (NX, NYW), ((0, 8), (1, 4)), -0.2, 0.2), 0.0, 2.0),
        "extrapolated": centred(keys[1], (NX, NYW), 1.0, 6.0, ((0, 8), (1, 4)), jnp.float32),
        "vis_dual": centred(keys[2], (VBLOCKS, 2, BW), 1.0, 6.0, ((0, 32),), jnp.float32),
        "tree_dual": centred(keys[3], (2, NX, NYW // 2), 1.0, 6.0, ((1, 8), (2, 4)), jnp.float32),
        "observed": centred(keys[4], (VBLOCKS, 2, BW), 1.0, 6.0, ((0, 32),), jnp.float32),
        "kernel": centred(keys[5], (BW, BW), BW ** -0.5, 0.5, (), jnp.float32),
        "block_index": touch_ends(jax.random.randint(keys[6], (VBLOCKS,), 0, UVB), jax.random.fold_in(keys[6], 1), 0, UVB - 1).astype(jnp.int32),
        "live_blocks": draw_live_blocks(jax.random.fold_in(keys[8], 71), 0),
    }


LOW_TAPS = (-0.010597401784997278, 0.032883011666982945, 0.030841381835986965, -0.18703481171888114, -0.02798376941698385, 0.6308807679295904, 0.7148465705525415, 0.23037781330885523)
HIGH_TAPS = tuple(((1.0 if position % 2 == 0 else -1.0) * LOW_TAPS[7 - position] for position in range(8)))

def analyse(coarse):
    approx = jnp.zeros((coarse.shape[0], coarse.shape[1] // 2), coarse.dtype)
    detail = jnp.zeros_like(approx)
    for position in range(8):
        rolled = jnp.roll(coarse, -position, axis=1)[:, ::2]
        approx = approx + LOW_TAPS[position] * rolled
        detail = detail + HIGH_TAPS[position] * rolled
    return (approx, detail)

def synthesise(approx, detail):
    width_rows = 2 * detail.shape[1]
    up_detail = jnp.zeros((detail.shape[0], width_rows), detail.dtype).at[:, ::2].set(detail)
    up_approx = jnp.zeros_like(up_detail).at[:, ::2].set(approx)
    result = jnp.zeros_like(up_detail)
    for position in range(8):
        result = result + LOW_TAPS[position] * jnp.roll(up_approx, position, axis=1)
        result = result + HIGH_TAPS[position] * jnp.roll(up_detail, position, axis=1)
    return result

def to_blocks(plane):
    shaped = plane.reshape(N_VIS, FACET, N_TILE, ROWS // BW, BW).transpose(0, 2, 1, 3, 4)
    return shaped.reshape(N_VIS * N_TILE, UVB, BW)

def from_blocks(blocks):
    shaped = blocks.reshape(N_VIS, N_TILE, FACET, ROWS // BW, BW).transpose(0, 2, 1, 3, 4)
    return shaped.reshape(NX, NYW)

def reference(image, extrapolated, vis_dual, tree_dual, observed, kernel, block_index, live_blocks):
    precise = lax.Precision.HIGHEST
    norm_scale = 1.0 / jnp.sqrt(jnp.float32(NX) * jnp.float32(NYW))
    spectrum = jnp.fft.fft(jnp.fft.fft(extrapolated, axis=0), axis=1)
    real_plane = jnp.real(spectrum) * norm_scale
    imag_plane = jnp.imag(spectrum) * norm_scale
    owner = (jnp.arange(VBLOCKS) // CAP).astype(jnp.int32)
    slot_pos = (jnp.arange(VBLOCKS) % CAP).astype(jnp.int32)
    chosen = jnp.stack([to_blocks(real_plane)[owner, block_index], to_blocks(imag_plane)[owner, block_index]], axis=1)
    model = jnp.einsum('ij,bsj->bsi', kernel, chosen, precision=precise)
    live_mask = (slot_pos < live_blocks[owner]).astype(extrapolated.dtype)[:, None, None]
    misfit = (vis_dual / 0.5 + model - observed) * live_mask
    radius = jnp.sqrt(2.0 * BW * jnp.sum(live_blocks.astype(extrapolated.dtype)))
    size_now = jnp.sqrt(jnp.sum(misfit * misfit))
    vis_next = 0.5 * misfit * (1.0 - radius / jnp.maximum(size_now, radius))
    contrib = jnp.einsum('ij,bsi->bsj', kernel, vis_next, precision=precise)
    segment_ids = owner * UVB + block_index
    summed = jax.ops.segment_sum(contrib, segment_ids, num_segments=N_VIS * N_TILE * UVB)
    summed = summed.reshape(N_VIS * N_TILE, UVB, 2, BW)
    grid_real = from_blocks(summed[:, :, 0, :])
    grid_imag = from_blocks(summed[:, :, 1, :])
    inverse = jnp.fft.ifft(jnp.fft.ifft(lax.complex(grid_real, grid_imag), axis=0), axis=1)
    data_term = jnp.real(inverse) * (jnp.float32(NX) * jnp.float32(NYW)) * norm_scale
    approx_one, detail_one = analyse(extrapolated)
    approx_two, detail_two = analyse(approx_one)
    child = tree_dual[0] + 0.5 * detail_one
    parent = tree_dual[1] + 0.5 * jnp.repeat(detail_two, 2, axis=1)
    factor = 1.0 / jnp.maximum(jnp.sqrt(child * child + parent * parent), 1.0)
    child_next = child * factor
    parent_next = parent * factor
    parent_sum = parent_next[:, 0::2] + parent_next[:, 1::2]
    level_one = synthesise(jnp.zeros_like(parent_sum), parent_sum)
    prior_term = synthesise(level_one, child_next)
    image_next = jnp.maximum(image - 0.5 * (data_term + prior_term), 0.0)
    return (image_next, vis_next, jnp.stack([child_next, parent_next]))
```

```python
import math

import jax
import jax.numpy as jnp
from jax import lax
from jax.sharding import PartitionSpec as P

LOW_TAPS = (
    -0.010597401784997278,
    0.032883011666982945,
    0.030841381835986965,
    -0.18703481171888114,
    -0.02798376941698385,
    0.6308807679295904,
    0.7148465705525415,
    0.23037781330885523,
)
HIGH_TAPS = tuple(
    ((1.0 if position % 2 == 0 else -1.0) * LOW_TAPS[7 - position] for position in range(8))
)
TWO_PI = 2.0 * math.pi


def shifted(block, axis, distance):
    devices = range(lax.axis_size(axis))
    route = [((i - distance) % len(devices), i) for i in devices]
    return lax.ppermute(block, axis, route)


def phase_table(left_ids, right_ids, period):
    turns = left_ids[:, None] * right_ids[None, :] % period
    angles = turns.astype(jnp.float32) * (TWO_PI / period)
    return (jnp.cos(angles), jnp.sin(angles))


def factor_pair(length):
    chosen_factor = 1
    for candidate in range(1, math.isqrt(length) + 1):
        if length % candidate == 0:
            chosen_factor = candidate
    return (chosen_factor, length // chosen_factor)


def complex_einsum(form, left_real, left_imag, table_cos, table_sin, real_only):
    precise = lax.Precision.HIGHEST
    real_part = jnp.einsum(form, left_real, table_cos, precision=precise)
    if left_imag is not None:
        real_part = real_part - jnp.einsum(form, left_imag, table_sin, precision=precise)
    if real_only:
        return (real_part, None)
    imag_part = jnp.einsum(form, left_real, table_sin, precision=precise)
    if left_imag is not None:
        imag_part = imag_part + jnp.einsum(form, left_imag, table_cos, precision=precise)
    return (imag_part * 0.0 + real_part, imag_part)


def transform_axis(real_in, imag_in, sign_value, along, real_only):
    length = real_in.shape[along]
    first_factor, second_factor = factor_pair(length)
    first_ids = jnp.arange(first_factor, dtype=jnp.int32)
    second_ids = jnp.arange(second_factor, dtype=jnp.int32)
    cos_first, sin_first = phase_table(first_ids, first_ids, first_factor)
    cos_twist, sin_twist = phase_table(first_ids, second_ids, length)
    cos_second, sin_second = phase_table(second_ids, second_ids, second_factor)
    sin_twist = sign_value * sin_twist
    if along == 0:
        other_len = real_in.shape[1]
        shape_in = (first_factor, second_factor, other_len)
        form_first = "abm,ca->cbm"
        form_second = "cbm,db->dcm"
        cos_twist = cos_twist[:, :, None]
        sin_twist = sin_twist[:, :, None]
        shape_out = (length, other_len)
    else:
        other_len = real_in.shape[0]
        shape_in = (other_len, first_factor, second_factor)
        form_first = "mab,ca->mcb"
        form_second = "mcb,db->mdc"
        cos_twist = cos_twist[None, :, :]
        sin_twist = sin_twist[None, :, :]
        shape_out = (other_len, length)
    shaped_real = real_in.reshape(shape_in)
    shaped_imag = None if imag_in is None else imag_in.reshape(shape_in)
    section_real, section_imag = complex_einsum(
        form_first, shaped_real, shaped_imag, cos_first, sign_value * sin_first, False
    )
    twisted_real = section_real * cos_twist - section_imag * sin_twist
    twisted_imag = section_real * sin_twist + section_imag * cos_twist
    out_real, out_imag = complex_einsum(
        form_second, twisted_real, twisted_imag, cos_second, sign_value * sin_second, real_only
    )
    if real_only:
        return (out_real.reshape(shape_out), None)
    return (out_real.reshape(shape_out), out_imag.reshape(shape_out))


def analyse_local(coarse):
    half_rows = coarse.shape[1] // 2
    next_rows = shifted(coarse[:, :6], "tile", -1)
    extended = jnp.concatenate([coarse, next_rows], axis=1)
    phases = [
        lax.slice_in_dim(extended, parity, extended.shape[1], 2, 1) for parity in range(2)
    ]
    approx = jnp.zeros((coarse.shape[0], half_rows), jnp.float32)
    detail = jnp.zeros_like(approx)
    for position in range(8):
        strided = lax.slice_in_dim(phases[position % 2], position // 2, position // 2 + half_rows, 1, 1)
        approx = approx + LOW_TAPS[position] * strided
        detail = detail + HIGH_TAPS[position] * strided
    return (approx, detail)


def upsample(ext_approx, ext_detail):
    out_rows = ext_detail.shape[1] - 3
    even_part = jnp.zeros((ext_detail.shape[0], out_rows), jnp.float32)
    odd_part = jnp.zeros_like(even_part)
    for lag_index in range(4):
        window_detail = ext_detail[:, 3 - lag_index : 3 - lag_index + out_rows]
        even_part = even_part + HIGH_TAPS[2 * lag_index] * window_detail
        odd_part = odd_part + HIGH_TAPS[2 * lag_index + 1] * window_detail
        if ext_approx is not None:
            window_approx = ext_approx[:, 3 - lag_index : 3 - lag_index + out_rows]
            even_part = even_part + LOW_TAPS[2 * lag_index] * window_approx
            odd_part = odd_part + LOW_TAPS[2 * lag_index + 1] * window_approx
    return jnp.stack([even_part, odd_part], axis=2).reshape(ext_detail.shape[0], 2 * out_rows)


def split_three(values):
    first = lax.reduce_precision(values, exponent_bits=8, mantissa_bits=7)
    rest = values - first
    second = lax.reduce_precision(rest, exponent_bits=8, mantissa_bits=7)
    third = rest - second
    pieces = [first, second, third]
    return jnp.concatenate([piece.astype(jnp.bfloat16) for piece in pieces], axis=-1)


def pick_rows(index, table):
    width = table.shape[1]
    selector = (index[:, None] == jnp.arange(table.shape[0], dtype=jnp.int32)[None, :]).astype(
        jnp.bfloat16
    )
    summed = jnp.dot(selector, split_three(table), preferred_element_type=jnp.float32)
    return summed[:, :width] + summed[:, width : 2 * width] + summed[:, 2 * width :]


def rows_to_grid(local_rows, values, row_count):
    groups, members, width = values.shape
    pieces = split_three(values)
    selector = (
        jnp.arange(row_count, dtype=jnp.int32)[None, :, None] == local_rows[:, None, :]
    ).astype(jnp.bfloat16)
    summed = jnp.einsum("gkb,gbc->gkc", selector, pieces, preferred_element_type=jnp.float32)
    summed = summed[..., :width] + summed[..., width : 2 * width] + summed[..., 2 * width :]
    return summed.reshape(groups * row_count, width)


def on_device(image, extrapolated, vis_dual, tree_dual, observed, kernel, block_index, live_blocks):
    precise = lax.Precision.HIGHEST
    slab_rows, slab_cols = image.shape
    n_vis = lax.axis_size("vis")
    n_tile = lax.axis_size("tile")
    vis_id = lax.axis_index("vis")
    tile_id = lax.axis_index("tile")
    len_rows = slab_rows * n_vis
    len_cols = slab_cols * n_tile
    block_width = kernel.shape[0]
    chunk = slab_cols // n_vis
    slot_count = vis_dual.shape[0]
    norm_scale = 1.0 / math.sqrt(len_rows * len_cols)
    columns = lax.all_to_all(extrapolated, "vis", split_axis=1, concat_axis=0, tiled=True)
    spec_real, spec_imag = transform_axis(columns, None, -1.0, 0, False)
    all_index = lax.all_gather(block_index, ("vis", "tile"), tiled=True)
    total_blocks = all_index.shape[0]
    owner = jnp.arange(total_blocks, dtype=jnp.int32) // slot_count
    per_row = slab_cols // block_width
    local_row = all_index // per_row
    row_of = (owner // n_tile) * slab_rows + local_row
    band_of = (owner % n_tile) * per_row + all_index % per_row
    col_ids = tile_id * slab_cols + vis_id * chunk + jnp.arange(chunk, dtype=jnp.int32)
    band_count = len_cols // block_width
    band_turns = (
        (jnp.arange(band_count, dtype=jnp.int32) * block_width)[:, None] * col_ids[None, :]
    ) % len_cols
    band_angles = band_turns.astype(jnp.float32) * (TWO_PI / len_cols)
    band_both = pick_rows(band_of, jnp.concatenate([jnp.cos(band_angles), jnp.sin(band_angles)], 1))
    band_cos = band_both[:, :chunk]
    band_sin = band_both[:, chunk:]
    cell_turns = (col_ids[:, None] * jnp.arange(block_width, dtype=jnp.int32)[None, :]) % len_cols
    cell_angles = cell_turns.astype(jnp.float32) * (TWO_PI / len_cols)
    cell_cos = jnp.cos(cell_angles)
    cell_sin = jnp.sin(cell_angles)
    picked_real = jnp.take(spec_real, row_of, axis=0)
    picked_imag = jnp.take(spec_imag, row_of, axis=0)
    twisted_real = picked_real * band_cos + picked_imag * band_sin
    twisted_imag = picked_imag * band_cos - picked_real * band_sin
    part_real = jnp.dot(twisted_real, cell_cos, precision=precise) + jnp.dot(
        twisted_imag, cell_sin, precision=precise
    )
    part_imag = jnp.dot(twisted_imag, cell_cos, precision=precise) - jnp.dot(
        twisted_real, cell_sin, precision=precise
    )
    partial = jnp.stack([part_real, part_imag], axis=1)
    partial = lax.all_to_all(partial, "vis", split_axis=0, concat_axis=0, tiled=True)
    partial = partial.reshape((n_vis, total_blocks // n_vis) + partial.shape[1:]).sum(axis=0)
    partial = lax.all_to_all(partial, "tile", split_axis=0, concat_axis=0, tiled=True)
    chosen = partial.reshape((n_tile, slot_count) + partial.shape[1:]).sum(axis=0) * norm_scale
    model = jnp.einsum("ij,csj->csi", kernel, chosen, precision=precise)
    live_mask = (jnp.arange(slot_count, dtype=jnp.int32) < live_blocks[0]).astype(jnp.float32)[
        :, None, None
    ]
    misfit = (vis_dual / 0.5 + model - observed) * live_mask
    totals = lax.psum((jnp.sum(misfit * misfit), jnp.sum(live_mask)), ("vis", "tile"))
    radius = jnp.sqrt(2.0 * block_width * totals[1])
    size_now = jnp.sqrt(totals[0])
    vis_next = 0.5 * misfit * (1.0 - radius / jnp.maximum(size_now, radius))
    contrib = jnp.einsum("ij,csi->csj", kernel, vis_next, precision=precise)
    every = lax.all_gather(contrib, "tile", tiled=True)
    every = lax.all_gather(every, "vis", tiled=True)
    back_real = jnp.dot(every[:, 0, :], cell_cos.T, precision=precise) - jnp.dot(
        every[:, 1, :], cell_sin.T, precision=precise
    )
    back_imag = jnp.dot(every[:, 0, :], cell_sin.T, precision=precise) + jnp.dot(
        every[:, 1, :], cell_cos.T, precision=precise
    )
    turned_real = back_real * band_cos - back_imag * band_sin
    turned_imag = back_real * band_sin + back_imag * band_cos
    turned = jnp.concatenate([turned_real, turned_imag], axis=1)
    turned = turned.reshape(n_vis, total_blocks // n_vis, 2 * chunk)
    gridded = rows_to_grid(local_row.reshape(n_vis, total_blocks // n_vis), turned, slab_rows)
    pixel_real, unused_part = transform_axis(gridded[:, :chunk], gridded[:, chunk:], 1.0, 0, True)
    data_term = (
        lax.all_to_all(pixel_real, "vis", split_axis=0, concat_axis=1, tiled=True) * norm_scale
    )
    approx_one, detail_one = analyse_local(extrapolated)
    approx_two, detail_two = analyse_local(approx_one)
    child = tree_dual[0] + 0.5 * detail_one
    parent = tree_dual[1] + 0.5 * jnp.repeat(detail_two, 2, axis=1)
    factor = 1.0 / jnp.maximum(jnp.sqrt(child * child + parent * parent), 1.0)
    child_next = child * factor
    parent_next = parent * factor
    parent_sum = parent_next[:, 0::2] + parent_next[:, 1::2]
    parent_tail = shifted(parent_sum[:, -3:], "tile", 1)
    level_one = upsample(None, jnp.concatenate([parent_tail, parent_sum], axis=1))
    both_tails = shifted(jnp.stack([level_one[:, -3:], child_next[:, -3:]]), "tile", 1)
    prior_term = upsample(
        jnp.concatenate([both_tails[0], level_one], axis=1),
        jnp.concatenate([both_tails[1], child_next], axis=1),
    )
    image_next = jnp.maximum(image - 0.5 * (data_term + prior_term), 0.0)
    return (image_next, vis_next, jnp.stack([child_next, parent_next]))


def solution(mesh):
    return jax.shard_map(
        on_device,
        mesh=mesh,
        in_specs=(
            P("vis", "tile"),
            P("vis", "tile"),
            P(("vis", "tile"), None, None),
            P(None, "vis", "tile"),
            P(("vis", "tile"), None, None),
            P(),
            P(("vis", "tile")),
            P(("vis", "tile")),
        ),
        out_specs=(P("vis", "tile"), P(("vis", "tile"), None, None), P(None, "vis", "tile")),
        check_vma=False,
    )
```

```python
import math

import jax
import jax.numpy as jnp
from jax import lax
from jax.sharding import PartitionSpec as P

LOW_TAPS = (
    -0.010597401784997278,
    0.032883011666982945,
    0.030841381835986965,
    -0.18703481171888114,
    -0.02798376941698385,
    0.6308807679295904,
    0.7148465705525415,
    0.23037781330885523,
)
HIGH_TAPS = tuple(
    ((1.0 if position % 2 == 0 else -1.0) * LOW_TAPS[7 - position] for position in range(8))
)
TWO_PI = 2.0 * math.pi


def shifted(block, axis, distance):
    devices = range(lax.axis_size(axis))
    route = [((i - distance) % len(devices), i) for i in devices]
    return lax.ppermute(block, axis, route)


def phase_table(left_ids, right_ids, period):
    turns = left_ids[:, None] * right_ids[None, :] % period
    angles = turns.astype(jnp.float32) * (TWO_PI / period)
    return (jnp.cos(angles), jnp.sin(angles))


def factor_pair(length):
    chosen_factor = 1
    for candidate in range(1, math.isqrt(length) + 1):
        if length % candidate == 0:
            chosen_factor = candidate
    return (chosen_factor, length // chosen_factor)


def complex_einsum(form, left_real, left_imag, table_cos, table_sin, real_only):
    precise = lax.Precision.HIGHEST
    real_part = jnp.einsum(form, left_real, table_cos, precision=precise)
    if left_imag is not None:
        real_part = real_part - jnp.einsum(form, left_imag, table_sin, precision=precise)
    if real_only:
        return (real_part, None)
    imag_part = jnp.einsum(form, left_real, table_sin, precision=precise)
    if left_imag is not None:
        imag_part = imag_part + jnp.einsum(form, left_imag, table_cos, precision=precise)
    return (imag_part * 0.0 + real_part, imag_part)


def transform_axis(real_in, imag_in, sign_value, along, real_only):
    length = real_in.shape[along]
    first_factor, second_factor = factor_pair(length)
    first_ids = jnp.arange(first_factor, dtype=jnp.int32)
    second_ids = jnp.arange(second_factor, dtype=jnp.int32)
    cos_first, sin_first = phase_table(first_ids, first_ids, first_factor)
    cos_twist, sin_twist = phase_table(first_ids, second_ids, length)
    cos_second, sin_second = phase_table(second_ids, second_ids, second_factor)
    sin_twist = sign_value * sin_twist
    if along == 0:
        other_len = real_in.shape[1]
        shape_in = (first_factor, second_factor, other_len)
        form_first = "abm,ca->cbm"
        form_second = "cbm,db->dcm"
        cos_twist = cos_twist[:, :, None]
        sin_twist = sin_twist[:, :, None]
        shape_out = (length, other_len)
    else:
        other_len = real_in.shape[0]
        shape_in = (other_len, first_factor, second_factor)
        form_first = "mab,ca->mcb"
        form_second = "mcb,db->mdc"
        cos_twist = cos_twist[None, :, :]
        sin_twist = sin_twist[None, :, :]
        shape_out = (other_len, length)
    shaped_real = real_in.reshape(shape_in)
    shaped_imag = None if imag_in is None else imag_in.reshape(shape_in)
    section_real, section_imag = complex_einsum(
        form_first, shaped_real, shaped_imag, cos_first, sign_value * sin_first, False
    )
    twisted_real = section_real * cos_twist - section_imag * sin_twist
    twisted_imag = section_real * sin_twist + section_imag * cos_twist
    out_real, out_imag = complex_einsum(
        form_second, twisted_real, twisted_imag, cos_second, sign_value * sin_second, real_only
    )
    if real_only:
        return (out_real.reshape(shape_out), None)
    return (out_real.reshape(shape_out), out_imag.reshape(shape_out))


def analyse_local(coarse):
    half_rows = coarse.shape[1] // 2
    next_rows = shifted(coarse[:, :6], "tile", -1)
    extended = jnp.concatenate([coarse, next_rows], axis=1)
    phases = [
        lax.slice_in_dim(extended, parity, extended.shape[1], 2, 1) for parity in range(2)
    ]
    approx = jnp.zeros((coarse.shape[0], half_rows), jnp.float32)
    detail = jnp.zeros_like(approx)
    for position in range(8):
        strided = lax.slice_in_dim(phases[position % 2], position // 2, position // 2 + half_rows, 1, 1)
        approx = approx + LOW_TAPS[position] * strided
        detail = detail + HIGH_TAPS[position] * strided
    return (approx, detail)


def upsample(ext_approx, ext_detail):
    out_rows = ext_detail.shape[1] - 3
    even_part = jnp.zeros((ext_detail.shape[0], out_rows), jnp.float32)
    odd_part = jnp.zeros_like(even_part)
    for lag_index in range(4):
        window_detail = ext_detail[:, 3 - lag_index : 3 - lag_index + out_rows]
        even_part = even_part + HIGH_TAPS[2 * lag_index] * window_detail
        odd_part = odd_part + HIGH_TAPS[2 * lag_index + 1] * window_detail
        if ext_approx is not None:
            window_approx = ext_approx[:, 3 - lag_index : 3 - lag_index + out_rows]
            even_part = even_part + LOW_TAPS[2 * lag_index] * window_approx
            odd_part = odd_part + LOW_TAPS[2 * lag_index + 1] * window_approx
    return jnp.stack([even_part, odd_part], axis=2).reshape(ext_detail.shape[0], 2 * out_rows)


def split_three(values):
    first = lax.reduce_precision(values, exponent_bits=8, mantissa_bits=7)
    rest = values - first
    second = lax.reduce_precision(rest, exponent_bits=8, mantissa_bits=7)
    third = rest - second
    pieces = [first, second, third]
    return jnp.concatenate([piece.astype(jnp.bfloat16) for piece in pieces], axis=-1)


def pick_rows(index, table):
    width = table.shape[1]
    selector = (index[:, None] == jnp.arange(table.shape[0], dtype=jnp.int32)[None, :]).astype(
        jnp.bfloat16
    )
    summed = jnp.dot(selector, split_three(table), preferred_element_type=jnp.float32)
    return summed[:, :width] + summed[:, width : 2 * width] + summed[:, 2 * width :]


def rows_to_grid(local_rows, values, row_count):
    groups, members, width = values.shape
    pieces = split_three(values)
    selector = (
        jnp.arange(row_count, dtype=jnp.int32)[None, :, None] == local_rows[:, None, :]
    ).astype(jnp.bfloat16)
    summed = jnp.einsum("gkb,gbc->gkc", selector, pieces, preferred_element_type=jnp.float32)
    summed = summed[..., :width] + summed[..., width : 2 * width] + summed[..., 2 * width :]
    return summed.reshape(groups * row_count, width)


def on_device(image, extrapolated, vis_dual, tree_dual, observed, kernel, block_index, live_blocks):
    precise = lax.Precision.HIGHEST
    slab_rows, slab_cols = image.shape
    n_vis = lax.axis_size("vis")
    n_tile = lax.axis_size("tile")
    vis_id = lax.axis_index("vis")
    tile_id = lax.axis_index("tile")
    len_rows = slab_rows * n_vis
    len_cols = slab_cols * n_tile
    block_width = kernel.shape[0]
    chunk = slab_cols // n_vis
    slot_count = vis_dual.shape[0]
    norm_scale = 1.0 / math.sqrt(len_rows * len_cols)
    columns = lax.all_to_all(extrapolated, "vis", split_axis=1, concat_axis=0, tiled=True)
    spec_real, spec_imag = transform_axis(columns, None, -1.0, 0, False)
    all_index = lax.all_gather(block_index.astype(jnp.float32), ("vis", "tile"), tiled=True)
    all_index = all_index.astype(jnp.int32)
    total_blocks = all_index.shape[0]
    owner = jnp.arange(total_blocks, dtype=jnp.int32) // slot_count
    per_row = slab_cols // block_width
    local_row = all_index // per_row
    row_of = (owner // n_tile) * slab_rows + local_row
    band_of = (owner % n_tile) * per_row + all_index % per_row
    col_ids = tile_id * slab_cols + vis_id * chunk + jnp.arange(chunk, dtype=jnp.int32)
    band_count = len_cols // block_width
    band_turns = (
        (jnp.arange(band_count, dtype=jnp.int32) * block_width)[:, None] * col_ids[None, :]
    ) % len_cols
    band_angles = band_turns.astype(jnp.float32) * (TWO_PI / len_cols)
    band_both = pick_rows(band_of, jnp.concatenate([jnp.cos(band_angles), jnp.sin(band_angles)], 1))
    band_cos = band_both[:, :chunk]
    band_sin = band_both[:, chunk:]
    cell_turns = (col_ids[:, None] * jnp.arange(block_width, dtype=jnp.int32)[None, :]) % len_cols
    cell_angles = cell_turns.astype(jnp.float32) * (TWO_PI / len_cols)
    cell_cos = jnp.cos(cell_angles)
    cell_sin = jnp.sin(cell_angles)
    picked_real = jnp.take(spec_real, row_of, axis=0)
    picked_imag = jnp.take(spec_imag, row_of, axis=0)
    twisted_real = picked_real * band_cos + picked_imag * band_sin
    twisted_imag = picked_imag * band_cos - picked_real * band_sin
    part_real = jnp.dot(twisted_real, cell_cos, precision=precise) + jnp.dot(
        twisted_imag, cell_sin, precision=precise
    )
    part_imag = jnp.dot(twisted_imag, cell_cos, precision=precise) - jnp.dot(
        twisted_real, cell_sin, precision=precise
    )
    partial = jnp.stack([part_real, part_imag], axis=1)
    partial = lax.psum_scatter(partial, "vis", scatter_dimension=0, tiled=True)
    chosen = lax.psum_scatter(partial, "tile", scatter_dimension=0, tiled=True) * norm_scale
    model = jnp.einsum("ij,csj->csi", kernel, chosen, precision=precise)
    live_mask = (jnp.arange(slot_count, dtype=jnp.int32) < live_blocks[0]).astype(jnp.float32)[
        :, None, None
    ]
    misfit = (vis_dual / 0.5 + model - observed) * live_mask
    totals = lax.psum((jnp.sum(misfit * misfit), jnp.sum(live_mask)), ("vis", "tile"))
    radius = jnp.sqrt(2.0 * block_width * totals[1])
    size_now = jnp.sqrt(totals[0])
    vis_next = 0.5 * misfit * (1.0 - radius / jnp.maximum(size_now, radius))
    contrib = jnp.einsum("ij,csi->csj", kernel, vis_next, precision=precise)
    every = lax.all_gather(contrib, "tile", tiled=True)
    every = lax.all_gather(every, "vis", tiled=True)
    back_real = jnp.dot(every[:, 0, :], cell_cos.T, precision=precise) - jnp.dot(
        every[:, 1, :], cell_sin.T, precision=precise
    )
    back_imag = jnp.dot(every[:, 0, :], cell_sin.T, precision=precise) + jnp.dot(
        every[:, 1, :], cell_cos.T, precision=precise
    )
    turned_real = back_real * band_cos - back_imag * band_sin
    turned_imag = back_real * band_sin + back_imag * band_cos
    turned = jnp.concatenate([turned_real, turned_imag], axis=1)
    turned = turned.reshape(n_vis, total_blocks // n_vis, 2 * chunk)
    gridded = rows_to_grid(local_row.reshape(n_vis, total_blocks // n_vis), turned, slab_rows)
    pixel_real, unused_part = transform_axis(gridded[:, :chunk], gridded[:, chunk:], 1.0, 0, True)
    data_term = (
        lax.all_to_all(pixel_real, "vis", split_axis=0, concat_axis=1, tiled=True) * norm_scale
    )
    approx_one, detail_one = analyse_local(extrapolated)
    approx_two, detail_two = analyse_local(approx_one)
    child = tree_dual[0] + 0.5 * detail_one
    parent = tree_dual[1] + 0.5 * jnp.repeat(detail_two, 2, axis=1)
    factor = 1.0 / jnp.maximum(jnp.sqrt(child * child + parent * parent), 1.0)
    child_next = child * factor
    parent_next = parent * factor
    parent_sum = parent_next[:, 0::2] + parent_next[:, 1::2]
    parent_tail = shifted(parent_sum[:, -3:], "tile", 1)
    level_one = upsample(None, jnp.concatenate([parent_tail, parent_sum], axis=1))
    both_tails = shifted(jnp.stack([level_one[:, -3:], child_next[:, -3:]]), "tile", 1)
    prior_term = upsample(
        jnp.concatenate([both_tails[0], level_one], axis=1),
        jnp.concatenate([both_tails[1], child_next], axis=1),
    )
    image_next = jnp.maximum(image - 0.5 * (data_term + prior_term), 0.0)
    return (image_next, vis_next, jnp.stack([child_next, parent_next]))


def solution(mesh):
    return jax.shard_map(
        on_device,
        mesh=mesh,
        in_specs=(
            P("vis", "tile"),
            P("vis", "tile"),
            P(("vis", "tile"), None, None),
            P(None, "vis", "tile"),
            P(("vis", "tile"), None, None),
            P(),
            P(("vis", "tile")),
            P(("vis", "tile")),
        ),
        out_specs=(P("vis", "tile"), P(("vis", "tile"), None, None), P(None, "vis", "tile")),
        check_vma=False,
    )
```

```python
import math

import jax
import jax.numpy as jnp
from jax import lax
from jax.sharding import PartitionSpec as P

LOW_TAPS = (
    -0.010597401784997278,
    0.032883011666982945,
    0.030841381835986965,
    -0.18703481171888114,
    -0.02798376941698385,
    0.6308807679295904,
    0.7148465705525415,
    0.23037781330885523,
)
HIGH_TAPS = tuple(
    ((1.0 if position % 2 == 0 else -1.0) * LOW_TAPS[7 - position] for position in range(8))
)
TWO_PI = 2.0 * math.pi


def shifted(block, axis, distance):
    devices = range(lax.axis_size(axis))
    route = [((i - distance) % len(devices), i) for i in devices]
    return lax.ppermute(block, axis, route)


def phase_table(left_ids, right_ids, period):
    turns = left_ids[:, None] * right_ids[None, :] % period
    angles = turns.astype(jnp.float32) * (TWO_PI / period)
    return (jnp.cos(angles), jnp.sin(angles))


def factor_pair(length):
    chosen_factor = 1
    for candidate in range(1, math.isqrt(length) + 1):
        if length % candidate == 0:
            chosen_factor = candidate
    return (chosen_factor, length // chosen_factor)


def complex_einsum(form, left_real, left_imag, table_cos, table_sin, real_only):
    precise = lax.Precision.HIGHEST
    real_part = jnp.einsum(form, left_real, table_cos, precision=precise)
    if left_imag is not None:
        real_part = real_part - jnp.einsum(form, left_imag, table_sin, precision=precise)
    if real_only:
        return (real_part, None)
    imag_part = jnp.einsum(form, left_real, table_sin, precision=precise)
    if left_imag is not None:
        imag_part = imag_part + jnp.einsum(form, left_imag, table_cos, precision=precise)
    return (imag_part * 0.0 + real_part, imag_part)


def transform_axis(real_in, imag_in, sign_value, along, real_only):
    length = real_in.shape[along]
    first_factor, second_factor = factor_pair(length)
    first_ids = jnp.arange(first_factor, dtype=jnp.int32)
    second_ids = jnp.arange(second_factor, dtype=jnp.int32)
    cos_first, sin_first = phase_table(first_ids, first_ids, first_factor)
    cos_twist, sin_twist = phase_table(first_ids, second_ids, length)
    cos_second, sin_second = phase_table(second_ids, second_ids, second_factor)
    sin_twist = sign_value * sin_twist
    if along == 0:
        other_len = real_in.shape[1]
        shape_in = (first_factor, second_factor, other_len)
        form_first = "abm,ca->cbm"
        form_second = "cbm,db->dcm"
        cos_twist = cos_twist[:, :, None]
        sin_twist = sin_twist[:, :, None]
        shape_out = (length, other_len)
    else:
        other_len = real_in.shape[0]
        shape_in = (other_len, first_factor, second_factor)
        form_first = "mab,ca->mcb"
        form_second = "mcb,db->mdc"
        cos_twist = cos_twist[None, :, :]
        sin_twist = sin_twist[None, :, :]
        shape_out = (other_len, length)
    shaped_real = real_in.reshape(shape_in)
    shaped_imag = None if imag_in is None else imag_in.reshape(shape_in)
    section_real, section_imag = complex_einsum(
        form_first, shaped_real, shaped_imag, cos_first, sign_value * sin_first, False
    )
    twisted_real = section_real * cos_twist - section_imag * sin_twist
    twisted_imag = section_real * sin_twist + section_imag * cos_twist
    out_real, out_imag = complex_einsum(
        form_second, twisted_real, twisted_imag, cos_second, sign_value * sin_second, real_only
    )
    if real_only:
        return (out_real.reshape(shape_out), None)
    return (out_real.reshape(shape_out), out_imag.reshape(shape_out))


def analyse_local(coarse):
    half_rows = coarse.shape[1] // 2
    next_rows = shifted(coarse[:, :6], "tile", -1)
    extended = jnp.concatenate([coarse, next_rows], axis=1)
    phases = [
        lax.slice_in_dim(extended, parity, extended.shape[1], 2, 1) for parity in range(2)
    ]
    approx = jnp.zeros((coarse.shape[0], half_rows), jnp.float32)
    detail = jnp.zeros_like(approx)
    for position in range(8):
        strided = lax.slice_in_dim(phases[position % 2], position // 2, position // 2 + half_rows, 1, 1)
        approx = approx + LOW_TAPS[position] * strided
        detail = detail + HIGH_TAPS[position] * strided
    return (approx, detail)


def upsample(ext_approx, ext_detail):
    out_rows = ext_detail.shape[1] - 3
    even_part = jnp.zeros((ext_detail.shape[0], out_rows), jnp.float32)
    odd_part = jnp.zeros_like(even_part)
    for lag_index in range(4):
        window_detail = ext_detail[:, 3 - lag_index : 3 - lag_index + out_rows]
        even_part = even_part + HIGH_TAPS[2 * lag_index] * window_detail
        odd_part = odd_part + HIGH_TAPS[2 * lag_index + 1] * window_detail
        if ext_approx is not None:
            window_approx = ext_approx[:, 3 - lag_index : 3 - lag_index + out_rows]
            even_part = even_part + LOW_TAPS[2 * lag_index] * window_approx
            odd_part = odd_part + LOW_TAPS[2 * lag_index + 1] * window_approx
    return jnp.stack([even_part, odd_part], axis=2).reshape(ext_detail.shape[0], 2 * out_rows)


def split_three(values):
    first = lax.reduce_precision(values, exponent_bits=8, mantissa_bits=7)
    rest = values - first
    second = lax.reduce_precision(rest, exponent_bits=8, mantissa_bits=7)
    third = rest - second
    pieces = [first, second, third]
    return jnp.concatenate([piece.astype(jnp.bfloat16) for piece in pieces], axis=-1)


def pick_rows(index, table):
    width = table.shape[1]
    selector = (index[:, None] == jnp.arange(table.shape[0], dtype=jnp.int32)[None, :]).astype(
        jnp.bfloat16
    )
    summed = jnp.dot(selector, split_three(table), preferred_element_type=jnp.float32)
    return summed[:, :width] + summed[:, width : 2 * width] + summed[:, 2 * width :]


def rows_to_grid(local_rows, values, row_count):
    groups, members, width = values.shape
    pieces = split_three(values)
    selector = (
        jnp.arange(row_count, dtype=jnp.int32)[None, :, None] == local_rows[:, None, :]
    ).astype(jnp.bfloat16)
    summed = jnp.einsum("gkb,gbc->gkc", selector, pieces, preferred_element_type=jnp.float32)
    summed = summed[..., :width] + summed[..., width : 2 * width] + summed[..., 2 * width :]
    return summed.reshape(groups * row_count, width)


def on_device(image, extrapolated, vis_dual, tree_dual, observed, kernel, block_index, live_blocks):
    precise = lax.Precision.HIGHEST
    slab_rows, slab_cols = image.shape
    n_vis = lax.axis_size("vis")
    n_tile = lax.axis_size("tile")
    vis_id = lax.axis_index("vis")
    tile_id = lax.axis_index("tile")
    len_rows = slab_rows * n_vis
    len_cols = slab_cols * n_tile
    block_width = kernel.shape[0]
    chunk = slab_cols // n_vis
    slot_count = vis_dual.shape[0]
    norm_scale = 1.0 / math.sqrt(len_rows * len_cols)
    columns = lax.all_to_all(extrapolated, "vis", split_axis=1, concat_axis=0, tiled=True)
    spec_real, spec_imag = transform_axis(columns, None, -1.0, 0, False)
    all_index = lax.all_gather(block_index.astype(jnp.float32), ("vis", "tile"), tiled=True)
    all_index = all_index.astype(jnp.int32)
    total_blocks = all_index.shape[0]
    owner = jnp.arange(total_blocks, dtype=jnp.int32) // slot_count
    per_row = slab_cols // block_width
    local_row = all_index // per_row
    row_of = (owner // n_tile) * slab_rows + local_row
    band_of = (owner % n_tile) * per_row + all_index % per_row
    col_ids = tile_id * slab_cols + vis_id * chunk + jnp.arange(chunk, dtype=jnp.int32)
    band_count = len_cols // block_width
    band_turns = (
        (jnp.arange(band_count, dtype=jnp.int32) * block_width)[:, None] * col_ids[None, :]
    ) % len_cols
    band_angles = band_turns.astype(jnp.float32) * (TWO_PI / len_cols)
    band_both = pick_rows(band_of, jnp.concatenate([jnp.cos(band_angles), jnp.sin(band_angles)], 1))
    band_cos = band_both[:, :chunk]
    band_sin = band_both[:, chunk:]
    cell_turns = (col_ids[:, None] * jnp.arange(block_width, dtype=jnp.int32)[None, :]) % len_cols
    cell_angles = cell_turns.astype(jnp.float32) * (TWO_PI / len_cols)
    cell_cos = jnp.cos(cell_angles)
    cell_sin = jnp.sin(cell_angles)
    picked_real = jnp.take(spec_real, row_of, axis=0)
    picked_imag = jnp.take(spec_imag, row_of, axis=0)
    twisted_real = picked_real * band_cos + picked_imag * band_sin
    twisted_imag = picked_imag * band_cos - picked_real * band_sin
    part_real = jnp.dot(twisted_real, cell_cos, precision=precise) + jnp.dot(
        twisted_imag, cell_sin, precision=precise
    )
    part_imag = jnp.dot(twisted_imag, cell_cos, precision=precise) - jnp.dot(
        twisted_real, cell_sin, precision=precise
    )
    partial = jnp.stack([part_real, part_imag], axis=1)
    partial = lax.psum_scatter(partial, "vis", scatter_dimension=0, tiled=True)
    chosen = lax.psum_scatter(partial, "tile", scatter_dimension=0, tiled=True) * norm_scale
    approx_one, detail_one = analyse_local(extrapolated)
    approx_two, detail_two = analyse_local(approx_one)
    child = tree_dual[0] + 0.5 * detail_one
    parent = tree_dual[1] + 0.5 * jnp.repeat(detail_two, 2, axis=1)
    factor = 1.0 / jnp.maximum(jnp.sqrt(child * child + parent * parent), 1.0)
    child_next = child * factor
    parent_next = parent * factor
    parent_sum = parent_next[:, 0::2] + parent_next[:, 1::2]
    parent_tail = shifted(parent_sum[:, -3:], "tile", 1)
    level_one = upsample(None, jnp.concatenate([parent_tail, parent_sum], axis=1))
    both_tails = shifted(jnp.stack([level_one[:, -3:], child_next[:, -3:]]), "tile", 1)
    prior_term = upsample(
        jnp.concatenate([both_tails[0], level_one], axis=1),
        jnp.concatenate([both_tails[1], child_next], axis=1),
    )
    chosen, child_next, parent_next, prior_term = lax.optimization_barrier(
        (chosen, child_next, parent_next, prior_term)
    )
    model = jnp.einsum("ij,csj->csi", kernel, chosen, precision=precise)
    live_mask = (jnp.arange(slot_count, dtype=jnp.int32) < live_blocks[0]).astype(jnp.float32)[
        :, None, None
    ]
    misfit = (vis_dual / 0.5 + model - observed) * live_mask
    totals = lax.psum((jnp.sum(misfit * misfit), jnp.sum(live_mask)), ("vis", "tile"))
    radius = jnp.sqrt(2.0 * block_width * totals[1])
    size_now = jnp.sqrt(totals[0])
    vis_next = 0.5 * misfit * (1.0 - radius / jnp.maximum(size_now, radius))
    contrib = jnp.einsum("ij,csi->csj", kernel, vis_next, precision=precise)
    every = lax.all_gather(contrib, "tile", tiled=True)
    every = lax.all_gather(every, "vis", tiled=True)
    back_real = jnp.dot(every[:, 0, :], cell_cos.T, precision=precise) - jnp.dot(
        every[:, 1, :], cell_sin.T, precision=precise
    )
    back_imag = jnp.dot(every[:, 0, :], cell_sin.T, precision=precise) + jnp.dot(
        every[:, 1, :], cell_cos.T, precision=precise
    )
    turned_real = back_real * band_cos - back_imag * band_sin
    turned_imag = back_real * band_sin + back_imag * band_cos
    turned = jnp.concatenate([turned_real, turned_imag], axis=1)
    turned = turned.reshape(n_vis, total_blocks // n_vis, 2 * chunk)
    gridded = rows_to_grid(local_row.reshape(n_vis, total_blocks // n_vis), turned, slab_rows)
    pixel_real, unused_part = transform_axis(gridded[:, :chunk], gridded[:, chunk:], 1.0, 0, True)
    data_term = (
        lax.all_to_all(pixel_real, "vis", split_axis=0, concat_axis=1, tiled=True) * norm_scale
    )
    image_next = jnp.maximum(image - 0.5 * (data_term + prior_term), 0.0)
    return (image_next, vis_next, jnp.stack([child_next, parent_next]))


def solution(mesh):
    return jax.shard_map(
        on_device,
        mesh=mesh,
        in_specs=(
            P("vis", "tile"),
            P("vis", "tile"),
            P(("vis", "tile"), None, None),
            P(None, "vis", "tile"),
            P(("vis", "tile"), None, None),
            P(),
            P(("vis", "tile")),
            P(("vis", "tile")),
        ),
        out_specs=(P("vis", "tile"), P(("vis", "tile"), None, None), P(None, "vis", "tile")),
        check_vma=False,
    )
```

```python
import math

import jax
import jax.numpy as jnp
from jax import lax
from jax.sharding import PartitionSpec as P

LOW_TAPS = (
    -0.010597401784997278,
    0.032883011666982945,
    0.030841381835986965,
    -0.18703481171888114,
    -0.02798376941698385,
    0.6308807679295904,
    0.7148465705525415,
    0.23037781330885523,
)
HIGH_TAPS = tuple(
    ((1.0 if position % 2 == 0 else -1.0) * LOW_TAPS[7 - position] for position in range(8))
)
TWO_PI = 2.0 * math.pi


def shifted(block, axis, distance):
    devices = range(lax.axis_size(axis))
    route = [((i - distance) % len(devices), i) for i in devices]
    return lax.ppermute(block, axis, route)


def phase_table(left_ids, right_ids, period):
    turns = left_ids[:, None] * right_ids[None, :] % period
    angles = turns.astype(jnp.float32) * (TWO_PI / period)
    return (jnp.cos(angles), jnp.sin(angles))


def factor_pair(length):
    chosen_factor = 1
    for candidate in range(1, math.isqrt(length) + 1):
        if length % candidate == 0:
            chosen_factor = candidate
    return (chosen_factor, length // chosen_factor)


def complex_einsum(form, left_real, left_imag, table_cos, table_sin, real_only):
    precise = lax.Precision.HIGHEST
    real_part = jnp.einsum(form, left_real, table_cos, precision=precise)
    if left_imag is not None:
        real_part = real_part - jnp.einsum(form, left_imag, table_sin, precision=precise)
    if real_only:
        return (real_part, None)
    imag_part = jnp.einsum(form, left_real, table_sin, precision=precise)
    if left_imag is not None:
        imag_part = imag_part + jnp.einsum(form, left_imag, table_cos, precision=precise)
    return (imag_part * 0.0 + real_part, imag_part)


def transform_axis(real_in, imag_in, sign_value, along, real_only):
    length = real_in.shape[along]
    first_factor, second_factor = factor_pair(length)
    first_ids = jnp.arange(first_factor, dtype=jnp.int32)
    second_ids = jnp.arange(second_factor, dtype=jnp.int32)
    cos_first, sin_first = phase_table(first_ids, first_ids, first_factor)
    cos_twist, sin_twist = phase_table(first_ids, second_ids, length)
    cos_second, sin_second = phase_table(second_ids, second_ids, second_factor)
    sin_twist = sign_value * sin_twist
    if along == 0:
        other_len = real_in.shape[1]
        shape_in = (first_factor, second_factor, other_len)
        form_first = "abm,ca->cbm"
        form_second = "cbm,db->dcm"
        cos_twist = cos_twist[:, :, None]
        sin_twist = sin_twist[:, :, None]
        shape_out = (length, other_len)
    else:
        other_len = real_in.shape[0]
        shape_in = (other_len, first_factor, second_factor)
        form_first = "mab,ca->mcb"
        form_second = "mcb,db->mdc"
        cos_twist = cos_twist[None, :, :]
        sin_twist = sin_twist[None, :, :]
        shape_out = (other_len, length)
    shaped_real = real_in.reshape(shape_in)
    shaped_imag = None if imag_in is None else imag_in.reshape(shape_in)
    section_real, section_imag = complex_einsum(
        form_first, shaped_real, shaped_imag, cos_first, sign_value * sin_first, False
    )
    twisted_real = section_real * cos_twist - section_imag * sin_twist
    twisted_imag = section_real * sin_twist + section_imag * cos_twist
    out_real, out_imag = complex_einsum(
        form_second, twisted_real, twisted_imag, cos_second, sign_value * sin_second, real_only
    )
    if real_only:
        return (out_real.reshape(shape_out), None)
    return (out_real.reshape(shape_out), out_imag.reshape(shape_out))


def analyse_local(coarse):
    half_rows = coarse.shape[1] // 2
    next_rows = shifted(coarse[:, :6], "tile", -1)
    extended = jnp.concatenate([coarse, next_rows], axis=1)
    phases = [
        lax.slice_in_dim(extended, parity, extended.shape[1], 2, 1) for parity in range(2)
    ]
    approx = jnp.zeros((coarse.shape[0], half_rows), jnp.float32)
    detail = jnp.zeros_like(approx)
    for position in range(8):
        strided = lax.slice_in_dim(phases[position % 2], position // 2, position // 2 + half_rows, 1, 1)
        approx = approx + LOW_TAPS[position] * strided
        detail = detail + HIGH_TAPS[position] * strided
    return (approx, detail)


def upsample(ext_approx, ext_detail):
    out_rows = ext_detail.shape[1] - 3
    even_part = jnp.zeros((ext_detail.shape[0], out_rows), jnp.float32)
    odd_part = jnp.zeros_like(even_part)
    for lag_index in range(4):
        window_detail = ext_detail[:, 3 - lag_index : 3 - lag_index + out_rows]
        even_part = even_part + HIGH_TAPS[2 * lag_index] * window_detail
        odd_part = odd_part + HIGH_TAPS[2 * lag_index + 1] * window_detail
        if ext_approx is not None:
            window_approx = ext_approx[:, 3 - lag_index : 3 - lag_index + out_rows]
            even_part = even_part + LOW_TAPS[2 * lag_index] * window_approx
            odd_part = odd_part + LOW_TAPS[2 * lag_index + 1] * window_approx
    return jnp.stack([even_part, odd_part], axis=2).reshape(ext_detail.shape[0], 2 * out_rows)


def split_three(values):
    first = lax.reduce_precision(values, exponent_bits=8, mantissa_bits=7)
    rest = values - first
    second = lax.reduce_precision(rest, exponent_bits=8, mantissa_bits=7)
    third = rest - second
    pieces = [first, second, third]
    return jnp.concatenate([piece.astype(jnp.bfloat16) for piece in pieces], axis=-1)


def pick_rows(index, table):
    width = table.shape[1]
    selector = (index[:, None] == jnp.arange(table.shape[0], dtype=jnp.int32)[None, :]).astype(
        jnp.bfloat16
    )
    summed = jnp.dot(selector, split_three(table), preferred_element_type=jnp.float32)
    return summed[:, :width] + summed[:, width : 2 * width] + summed[:, 2 * width :]


def rows_to_grid(local_rows, values, row_count):
    groups, members, width = values.shape
    pieces = split_three(values)
    selector = (
        jnp.arange(row_count, dtype=jnp.int32)[None, :, None] == local_rows[:, None, :]
    ).astype(jnp.bfloat16)
    summed = jnp.einsum("gkb,gbc->gkc", selector, pieces, preferred_element_type=jnp.float32)
    summed = summed[..., :width] + summed[..., width : 2 * width] + summed[..., 2 * width :]
    return summed.reshape(groups * row_count, width)


def on_device(image, extrapolated, vis_dual, tree_dual, observed, kernel, block_index, live_blocks):
    precise = lax.Precision.HIGHEST
    slab_rows, slab_cols = image.shape
    n_vis = lax.axis_size("vis")
    n_tile = lax.axis_size("tile")
    vis_id = lax.axis_index("vis")
    tile_id = lax.axis_index("tile")
    len_rows = slab_rows * n_vis
    len_cols = slab_cols * n_tile
    block_width = kernel.shape[0]
    chunk = slab_cols // n_vis
    slot_count = vis_dual.shape[0]
    norm_scale = 1.0 / math.sqrt(len_rows * len_cols)
    columns = lax.all_to_all(extrapolated, "vis", split_axis=1, concat_axis=0, tiled=True)
    spec_real, spec_imag = transform_axis(columns, None, -1.0, 0, False)
    all_index = lax.all_gather(block_index.astype(jnp.float32), ("vis", "tile"), tiled=True)
    all_index = all_index.astype(jnp.int32)
    total_blocks = all_index.shape[0]
    owner = jnp.arange(total_blocks, dtype=jnp.int32) // slot_count
    per_row = slab_cols // block_width
    local_row = all_index // per_row
    row_of = (owner // n_tile) * slab_rows + local_row
    band_of = (owner % n_tile) * per_row + all_index % per_row
    col_ids = tile_id * slab_cols + vis_id * chunk + jnp.arange(chunk, dtype=jnp.int32)
    band_count = len_cols // block_width
    band_turns = (
        (jnp.arange(band_count, dtype=jnp.int32) * block_width)[:, None] * col_ids[None, :]
    ) % len_cols
    band_angles = band_turns.astype(jnp.float32) * (TWO_PI / len_cols)
    band_both = pick_rows(band_of, jnp.concatenate([jnp.cos(band_angles), jnp.sin(band_angles)], 1))
    band_cos = band_both[:, :chunk]
    band_sin = band_both[:, chunk:]
    cell_turns = (col_ids[:, None] * jnp.arange(block_width, dtype=jnp.int32)[None, :]) % len_cols
    cell_angles = cell_turns.astype(jnp.float32) * (TWO_PI / len_cols)
    cell_cos = jnp.cos(cell_angles)
    cell_sin = jnp.sin(cell_angles)
    picked = jnp.take(jnp.concatenate([spec_real, spec_imag], axis=1), row_of, axis=0)
    picked_real = picked[:, :chunk]
    picked_imag = picked[:, chunk:]
    twisted_real = picked_real * band_cos + picked_imag * band_sin
    twisted_imag = picked_imag * band_cos - picked_real * band_sin
    part_real = jnp.dot(twisted_real, cell_cos, precision=precise) + jnp.dot(
        twisted_imag, cell_sin, precision=precise
    )
    part_imag = jnp.dot(twisted_imag, cell_cos, precision=precise) - jnp.dot(
        twisted_real, cell_sin, precision=precise
    )
    partial = jnp.stack([part_real, part_imag], axis=1)
    partial = lax.psum_scatter(partial, "vis", scatter_dimension=0, tiled=True)
    chosen = lax.psum_scatter(partial, "tile", scatter_dimension=0, tiled=True) * norm_scale
    model = jnp.einsum("ij,csj->csi", kernel, chosen, precision=precise)
    live_mask = (jnp.arange(slot_count, dtype=jnp.int32) < live_blocks[0]).astype(jnp.float32)[
        :, None, None
    ]
    misfit = (vis_dual / 0.5 + model - observed) * live_mask
    totals = lax.psum((jnp.sum(misfit * misfit), jnp.sum(live_mask)), ("vis", "tile"))
    radius = jnp.sqrt(2.0 * block_width * totals[1])
    size_now = jnp.sqrt(totals[0])
    vis_next = 0.5 * misfit * (1.0 - radius / jnp.maximum(size_now, radius))
    contrib = jnp.einsum("ij,csi->csj", kernel, vis_next, precision=precise)
    every = lax.all_gather(contrib, "tile", tiled=True)
    every = lax.all_gather(every, "vis", tiled=True)
    back_real = jnp.dot(every[:, 0, :], cell_cos.T, precision=precise) - jnp.dot(
        every[:, 1, :], cell_sin.T, precision=precise
    )
    back_imag = jnp.dot(every[:, 0, :], cell_sin.T, precision=precise) + jnp.dot(
        every[:, 1, :], cell_cos.T, precision=precise
    )
    turned_real = back_real * band_cos - back_imag * band_sin
    turned_imag = back_real * band_sin + back_imag * band_cos
    turned = jnp.concatenate([turned_real, turned_imag], axis=1)
    turned = turned.reshape(n_vis, total_blocks // n_vis, 2 * chunk)
    gridded = rows_to_grid(local_row.reshape(n_vis, total_blocks // n_vis), turned, slab_rows)
    pixel_real, unused_part = transform_axis(gridded[:, :chunk], gridded[:, chunk:], 1.0, 0, True)
    data_term = (
        lax.all_to_all(pixel_real, "vis", split_axis=0, concat_axis=1, tiled=True) * norm_scale
    )
    approx_one, detail_one = analyse_local(extrapolated)
    approx_two, detail_two = analyse_local(approx_one)
    child = tree_dual[0] + 0.5 * detail_one
    parent = tree_dual[1] + 0.5 * jnp.repeat(detail_two, 2, axis=1)
    factor = 1.0 / jnp.maximum(jnp.sqrt(child * child + parent * parent), 1.0)
    child_next = child * factor
    parent_next = parent * factor
    parent_sum = parent_next[:, 0::2] + parent_next[:, 1::2]
    parent_tail = shifted(parent_sum[:, -3:], "tile", 1)
    level_one = upsample(None, jnp.concatenate([parent_tail, parent_sum], axis=1))
    both_tails = shifted(jnp.stack([level_one[:, -3:], child_next[:, -3:]]), "tile", 1)
    prior_term = upsample(
        jnp.concatenate([both_tails[0], level_one], axis=1),
        jnp.concatenate([both_tails[1], child_next], axis=1),
    )
    image_next = jnp.maximum(image - 0.5 * (data_term + prior_term), 0.0)
    return (image_next, vis_next, jnp.stack([child_next, parent_next]))


def solution(mesh):
    return jax.shard_map(
        on_device,
        mesh=mesh,
        in_specs=(
            P("vis", "tile"),
            P("vis", "tile"),
            P(("vis", "tile"), None, None),
            P(None, "vis", "tile"),
            P(("vis", "tile"), None, None),
            P(),
            P(("vis", "tile")),
            P(("vis", "tile")),
        ),
        out_specs=(P("vis", "tile"), P(("vis", "tile"), None, None), P(None, "vis", "tile")),
        check_vma=False,
    )
```

```python
import math

import jax
import jax.numpy as jnp
from jax import lax
from jax.sharding import PartitionSpec as P

LOW_TAPS = (
    -0.010597401784997278,
    0.032883011666982945,
    0.030841381835986965,
    -0.18703481171888114,
    -0.02798376941698385,
    0.6308807679295904,
    0.7148465705525415,
    0.23037781330885523,
)
HIGH_TAPS = tuple(
    ((1.0 if position % 2 == 0 else -1.0) * LOW_TAPS[7 - position] for position in range(8))
)
TWO_PI = 2.0 * math.pi


def shifted(block, axis, distance):
    devices = range(lax.axis_size(axis))
    route = [((i - distance) % len(devices), i) for i in devices]
    return lax.ppermute(block, axis, route)


def phase_table(left_ids, right_ids, period):
    turns = left_ids[:, None] * right_ids[None, :] % period
    angles = turns.astype(jnp.float32) * (TWO_PI / period)
    return (jnp.cos(angles), jnp.sin(angles))


def factor_pair(length):
    chosen_factor = 1
    for candidate in range(1, math.isqrt(length) + 1):
        if length % candidate == 0:
            chosen_factor = candidate
    return (chosen_factor, length // chosen_factor)


def complex_einsum(form, left_real, left_imag, table_cos, table_sin, real_only):
    precise = lax.Precision.HIGHEST
    real_part = jnp.einsum(form, left_real, table_cos, precision=precise)
    if left_imag is not None:
        real_part = real_part - jnp.einsum(form, left_imag, table_sin, precision=precise)
    if real_only:
        return (real_part, None)
    imag_part = jnp.einsum(form, left_real, table_sin, precision=precise)
    if left_imag is not None:
        imag_part = imag_part + jnp.einsum(form, left_imag, table_cos, precision=precise)
    return (imag_part * 0.0 + real_part, imag_part)


def transform_axis(real_in, imag_in, sign_value, along, real_only):
    length = real_in.shape[along]
    first_factor, second_factor = factor_pair(length)
    first_ids = jnp.arange(first_factor, dtype=jnp.int32)
    second_ids = jnp.arange(second_factor, dtype=jnp.int32)
    cos_first, sin_first = phase_table(first_ids, first_ids, first_factor)
    cos_twist, sin_twist = phase_table(first_ids, second_ids, length)
    cos_second, sin_second = phase_table(second_ids, second_ids, second_factor)
    sin_twist = sign_value * sin_twist
    if along == 0:
        other_len = real_in.shape[1]
        shape_in = (first_factor, second_factor, other_len)
        form_first = "abm,ca->cbm"
        form_second = "cbm,db->dcm"
        cos_twist = cos_twist[:, :, None]
        sin_twist = sin_twist[:, :, None]
        shape_out = (length, other_len)
    else:
        other_len = real_in.shape[0]
        shape_in = (other_len, first_factor, second_factor)
        form_first = "mab,ca->mcb"
        form_second = "mcb,db->mdc"
        cos_twist = cos_twist[None, :, :]
        sin_twist = sin_twist[None, :, :]
        shape_out = (other_len, length)
    shaped_real = real_in.reshape(shape_in)
    shaped_imag = None if imag_in is None else imag_in.reshape(shape_in)
    section_real, section_imag = complex_einsum(
        form_first, shaped_real, shaped_imag, cos_first, sign_value * sin_first, False
    )
    twisted_real = section_real * cos_twist - section_imag * sin_twist
    twisted_imag = section_real * sin_twist + section_imag * cos_twist
    out_real, out_imag = complex_einsum(
        form_second, twisted_real, twisted_imag, cos_second, sign_value * sin_second, real_only
    )
    if real_only:
        return (out_real.reshape(shape_out), None)
    return (out_real.reshape(shape_out), out_imag.reshape(shape_out))


def analyse_local(coarse):
    half_rows = coarse.shape[1] // 2
    next_rows = shifted(coarse[:, :6], "tile", -1)
    extended = jnp.concatenate([coarse, next_rows], axis=1)
    phases = [
        lax.slice_in_dim(extended, parity, extended.shape[1], 2, 1) for parity in range(2)
    ]
    approx = jnp.zeros((coarse.shape[0], half_rows), jnp.float32)
    detail = jnp.zeros_like(approx)
    for position in range(8):
        strided = lax.slice_in_dim(phases[position % 2], position // 2, position // 2 + half_rows, 1, 1)
        approx = approx + LOW_TAPS[position] * strided
        detail = detail + HIGH_TAPS[position] * strided
    return (approx, detail)


def upsample(ext_approx, ext_detail):
    out_rows = ext_detail.shape[1] - 3
    even_part = jnp.zeros((ext_detail.shape[0], out_rows), jnp.float32)
    odd_part = jnp.zeros_like(even_part)
    for lag_index in range(4):
        window_detail = ext_detail[:, 3 - lag_index : 3 - lag_index + out_rows]
        even_part = even_part + HIGH_TAPS[2 * lag_index] * window_detail
        odd_part = odd_part + HIGH_TAPS[2 * lag_index + 1] * window_detail
        if ext_approx is not None:
            window_approx = ext_approx[:, 3 - lag_index : 3 - lag_index + out_rows]
            even_part = even_part + LOW_TAPS[2 * lag_index] * window_approx
            odd_part = odd_part + LOW_TAPS[2 * lag_index + 1] * window_approx
    return jnp.stack([even_part, odd_part], axis=2).reshape(ext_detail.shape[0], 2 * out_rows)


def split_three(values, axis):
    first = lax.reduce_precision(values, exponent_bits=8, mantissa_bits=7)
    rest = values - first
    second = lax.reduce_precision(rest, exponent_bits=8, mantissa_bits=7)
    third = rest - second
    pieces = [first, second, third]
    return jnp.concatenate([piece.astype(jnp.bfloat16) for piece in pieces], axis=axis)


def pick_rows(index, table):
    selector = (index[:, None] == jnp.arange(table.shape[0], dtype=jnp.int32)[None, :]).astype(
        jnp.bfloat16
    )
    selector = jnp.concatenate([selector] * 3, axis=1)
    return jnp.dot(selector, split_three(table, 0), preferred_element_type=jnp.float32)


def rows_to_grid(local_rows, values, row_count):
    groups, members, width = values.shape
    pieces = split_three(values, 1)
    selector = (
        jnp.arange(row_count, dtype=jnp.int32)[None, :, None] == local_rows[:, None, :]
    ).astype(jnp.bfloat16)
    selector = jnp.concatenate([selector] * 3, axis=2)
    summed = jnp.einsum("gkb,gbc->gkc", selector, pieces, preferred_element_type=jnp.float32)
    return summed.reshape(groups * row_count, width)


def on_device(image, extrapolated, vis_dual, tree_dual, observed, kernel, block_index, live_blocks):
    precise = lax.Precision.HIGHEST
    slab_rows, slab_cols = image.shape
    n_vis = lax.axis_size("vis")
    n_tile = lax.axis_size("tile")
    vis_id = lax.axis_index("vis")
    tile_id = lax.axis_index("tile")
    len_rows = slab_rows * n_vis
    len_cols = slab_cols * n_tile
    block_width = kernel.shape[0]
    chunk = slab_cols // n_vis
    slot_count = vis_dual.shape[0]
    norm_scale = 1.0 / math.sqrt(len_rows * len_cols)
    columns = lax.all_to_all(extrapolated, "vis", split_axis=1, concat_axis=0, tiled=True)
    spec_real, spec_imag = transform_axis(columns, None, -1.0, 0, False)
    all_index = lax.all_gather(block_index.astype(jnp.float32), ("vis", "tile"), tiled=True)
    all_index = all_index.astype(jnp.int32)
    total_blocks = all_index.shape[0]
    owner = jnp.arange(total_blocks, dtype=jnp.int32) // slot_count
    per_row = slab_cols // block_width
    local_row = all_index // per_row
    row_of = (owner // n_tile) * slab_rows + local_row
    band_of = (owner % n_tile) * per_row + all_index % per_row
    col_ids = tile_id * slab_cols + vis_id * chunk + jnp.arange(chunk, dtype=jnp.int32)
    band_count = len_cols // block_width
    band_turns = (
        (jnp.arange(band_count, dtype=jnp.int32) * block_width)[:, None] * col_ids[None, :]
    ) % len_cols
    band_angles = band_turns.astype(jnp.float32) * (TWO_PI / len_cols)
    band_both = pick_rows(band_of, jnp.concatenate([jnp.cos(band_angles), jnp.sin(band_angles)], 1))
    band_cos = band_both[:, :chunk]
    band_sin = band_both[:, chunk:]
    cell_turns = (col_ids[:, None] * jnp.arange(block_width, dtype=jnp.int32)[None, :]) % len_cols
    cell_angles = cell_turns.astype(jnp.float32) * (TWO_PI / len_cols)
    cell_cos = jnp.cos(cell_angles)
    cell_sin = jnp.sin(cell_angles)
    picked = jnp.take(jnp.concatenate([spec_real, spec_imag], axis=1), row_of, axis=0)
    picked_real = picked[:, :chunk]
    picked_imag = picked[:, chunk:]
    twisted_real = picked_real * band_cos + picked_imag * band_sin
    twisted_imag = picked_imag * band_cos - picked_real * band_sin
    part_real = jnp.dot(twisted_real, cell_cos, precision=precise) + jnp.dot(
        twisted_imag, cell_sin, precision=precise
    )
    part_imag = jnp.dot(twisted_imag, cell_cos, precision=precise) - jnp.dot(
        twisted_real, cell_sin, precision=precise
    )
    partial = jnp.stack([part_real, part_imag], axis=1)
    partial = lax.psum_scatter(partial, "vis", scatter_dimension=0, tiled=True)
    chosen = lax.psum_scatter(partial, "tile", scatter_dimension=0, tiled=True) * norm_scale
    model = jnp.einsum("ij,csj->csi", kernel, chosen, precision=precise)
    live_mask = (jnp.arange(slot_count, dtype=jnp.int32) < live_blocks[0]).astype(jnp.float32)[
        :, None, None
    ]
    misfit = (vis_dual / 0.5 + model - observed) * live_mask
    totals = lax.psum((jnp.sum(misfit * misfit), jnp.sum(live_mask)), ("vis", "tile"))
    radius = jnp.sqrt(2.0 * block_width * totals[1])
    size_now = jnp.sqrt(totals[0])
    vis_next = 0.5 * misfit * (1.0 - radius / jnp.maximum(size_now, radius))
    contrib = jnp.einsum("ij,csi->csj", kernel, vis_next, precision=precise)
    every = lax.all_gather(contrib, "tile", tiled=True)
    every = lax.all_gather(every, "vis", tiled=True)
    back_real = jnp.dot(every[:, 0, :], cell_cos.T, precision=precise) - jnp.dot(
        every[:, 1, :], cell_sin.T, precision=precise
    )
    back_imag = jnp.dot(every[:, 0, :], cell_sin.T, precision=precise) + jnp.dot(
        every[:, 1, :], cell_cos.T, precision=precise
    )
    turned_real = back_real * band_cos - back_imag * band_sin
    turned_imag = back_real * band_sin + back_imag * band_cos
    turned = jnp.concatenate([turned_real, turned_imag], axis=1)
    turned = turned.reshape(n_vis, total_blocks // n_vis, 2 * chunk)
    gridded = rows_to_grid(local_row.reshape(n_vis, total_blocks // n_vis), turned, slab_rows)
    pixel_real, unused_part = transform_axis(gridded[:, :chunk], gridded[:, chunk:], 1.0, 0, True)
    data_term = (
        lax.all_to_all(pixel_real, "vis", split_axis=0, concat_axis=1, tiled=True) * norm_scale
    )
    approx_one, detail_one = analyse_local(extrapolated)
    approx_two, detail_two = analyse_local(approx_one)
    child = tree_dual[0] + 0.5 * detail_one
    parent = tree_dual[1] + 0.5 * jnp.repeat(detail_two, 2, axis=1)
    factor = 1.0 / jnp.maximum(jnp.sqrt(child * child + parent * parent), 1.0)
    child_next = child * factor
    parent_next = parent * factor
    parent_sum = parent_next[:, 0::2] + parent_next[:, 1::2]
    parent_tail = shifted(parent_sum[:, -3:], "tile", 1)
    level_one = upsample(None, jnp.concatenate([parent_tail, parent_sum], axis=1))
    both_tails = shifted(jnp.stack([level_one[:, -3:], child_next[:, -3:]]), "tile", 1)
    prior_term = upsample(
        jnp.concatenate([both_tails[0], level_one], axis=1),
        jnp.concatenate([both_tails[1], child_next], axis=1),
    )
    image_next = jnp.maximum(image - 0.5 * (data_term + prior_term), 0.0)
    return (image_next, vis_next, jnp.stack([child_next, parent_next]))


def solution(mesh):
    return jax.shard_map(
        on_device,
        mesh=mesh,
        in_specs=(
            P("vis", "tile"),
            P("vis", "tile"),
            P(("vis", "tile"), None, None),
            P(None, "vis", "tile"),
            P(("vis", "tile"), None, None),
            P(),
            P(("vis", "tile")),
            P(("vis", "tile")),
        ),
        out_specs=(P("vis", "tile"), P(("vis", "tile"), None, None), P(None, "vis", "tile")),
        check_vma=False,
    )
```

```python
import math

import jax
import jax.numpy as jnp
from jax import lax
from jax.sharding import PartitionSpec as P

LOW_TAPS = (
    -0.010597401784997278,
    0.032883011666982945,
    0.030841381835986965,
    -0.18703481171888114,
    -0.02798376941698385,
    0.6308807679295904,
    0.7148465705525415,
    0.23037781330885523,
)
HIGH_TAPS = tuple(
    ((1.0 if position % 2 == 0 else -1.0) * LOW_TAPS[7 - position] for position in range(8))
)
TWO_PI = 2.0 * math.pi


def shifted(block, axis, distance):
    devices = range(lax.axis_size(axis))
    route = [((i - distance) % len(devices), i) for i in devices]
    return lax.ppermute(block, axis, route)


def phase_table(left_ids, right_ids, period):
    turns = left_ids[:, None] * right_ids[None, :] % period
    angles = turns.astype(jnp.float32) * (TWO_PI / period)
    return (jnp.cos(angles), jnp.sin(angles))


def factor_pair(length):
    chosen_factor = 1
    for candidate in range(1, math.isqrt(length) + 1):
        if length % candidate == 0:
            chosen_factor = candidate
    return (chosen_factor, length // chosen_factor)


def complex_einsum(form, left_real, left_imag, table_cos, table_sin, real_only):
    precise = lax.Precision.HIGHEST
    real_part = jnp.einsum(form, left_real, table_cos, precision=precise)
    if left_imag is not None:
        real_part = real_part - jnp.einsum(form, left_imag, table_sin, precision=precise)
    if real_only:
        return (real_part, None)
    imag_part = jnp.einsum(form, left_real, table_sin, precision=precise)
    if left_imag is not None:
        imag_part = imag_part + jnp.einsum(form, left_imag, table_cos, precision=precise)
    return (imag_part * 0.0 + real_part, imag_part)


def transform_axis(real_in, imag_in, sign_value, along, real_only):
    length = real_in.shape[along]
    first_factor, second_factor = factor_pair(length)
    first_ids = jnp.arange(first_factor, dtype=jnp.int32)
    second_ids = jnp.arange(second_factor, dtype=jnp.int32)
    cos_first, sin_first = phase_table(first_ids, first_ids, first_factor)
    cos_twist, sin_twist = phase_table(first_ids, second_ids, length)
    cos_second, sin_second = phase_table(second_ids, second_ids, second_factor)
    sin_twist = sign_value * sin_twist
    if along == 0:
        other_len = real_in.shape[1]
        shape_in = (first_factor, second_factor, other_len)
        form_first = "abm,ca->cbm"
        form_second = "cbm,db->dcm"
        cos_twist = cos_twist[:, :, None]
        sin_twist = sin_twist[:, :, None]
        shape_out = (length, other_len)
    else:
        other_len = real_in.shape[0]
        shape_in = (other_len, first_factor, second_factor)
        form_first = "mab,ca->mcb"
        form_second = "mcb,db->mdc"
        cos_twist = cos_twist[None, :, :]
        sin_twist = sin_twist[None, :, :]
        shape_out = (other_len, length)
    shaped_real = real_in.reshape(shape_in)
    shaped_imag = None if imag_in is None else imag_in.reshape(shape_in)
    section_real, section_imag = complex_einsum(
        form_first, shaped_real, shaped_imag, cos_first, sign_value * sin_first, False
    )
    twisted_real = section_real * cos_twist - section_imag * sin_twist
    twisted_imag = section_real * sin_twist + section_imag * cos_twist
    out_real, out_imag = complex_einsum(
        form_second, twisted_real, twisted_imag, cos_second, sign_value * sin_second, real_only
    )
    if real_only:
        return (out_real.reshape(shape_out), None)
    return (out_real.reshape(shape_out), out_imag.reshape(shape_out))


def analyse_local(coarse):
    half_rows = coarse.shape[1] // 2
    next_rows = shifted(coarse[:, :6], "tile", -1)
    extended = jnp.concatenate([coarse, next_rows], axis=1)
    phases = [
        lax.slice_in_dim(extended, parity, extended.shape[1], 2, 1) for parity in range(2)
    ]
    approx = jnp.zeros((coarse.shape[0], half_rows), jnp.float32)
    detail = jnp.zeros_like(approx)
    for position in range(8):
        strided = lax.slice_in_dim(phases[position % 2], position // 2, position // 2 + half_rows, 1, 1)
        approx = approx + LOW_TAPS[position] * strided
        detail = detail + HIGH_TAPS[position] * strided
    return (approx, detail)


def upsample(ext_approx, ext_detail):
    out_rows = ext_detail.shape[1] - 3
    even_part = jnp.zeros((ext_detail.shape[0], out_rows), jnp.float32)
    odd_part = jnp.zeros_like(even_part)
    for lag_index in range(4):
        window_detail = ext_detail[:, 3 - lag_index : 3 - lag_index + out_rows]
        even_part = even_part + HIGH_TAPS[2 * lag_index] * window_detail
        odd_part = odd_part + HIGH_TAPS[2 * lag_index + 1] * window_detail
        if ext_approx is not None:
            window_approx = ext_approx[:, 3 - lag_index : 3 - lag_index + out_rows]
            even_part = even_part + LOW_TAPS[2 * lag_index] * window_approx
            odd_part = odd_part + LOW_TAPS[2 * lag_index + 1] * window_approx
    return jnp.stack([even_part, odd_part], axis=2).reshape(ext_detail.shape[0], 2 * out_rows)


def split_three(values, axis):
    first = lax.reduce_precision(values, exponent_bits=8, mantissa_bits=7)
    rest = values - first
    second = lax.reduce_precision(rest, exponent_bits=8, mantissa_bits=7)
    third = rest - second
    pieces = [first, second, third]
    return jnp.concatenate([piece.astype(jnp.bfloat16) for piece in pieces], axis=axis)


def pick_rows(index, table):
    selector = (index[:, None] == jnp.arange(table.shape[0], dtype=jnp.int32)[None, :]).astype(
        jnp.bfloat16
    )
    selector = jnp.concatenate([selector] * 3, axis=1)
    return jnp.dot(selector, split_three(table, 0), preferred_element_type=jnp.float32)


def rows_to_grid(local_rows, values, row_count):
    groups, members, width = values.shape
    pieces = split_three(values, 1)
    selector = (
        jnp.arange(row_count, dtype=jnp.int32)[None, :, None] == local_rows[:, None, :]
    ).astype(jnp.bfloat16)
    selector = jnp.concatenate([selector] * 3, axis=2)
    summed = jnp.einsum("gkb,gbc->gkc", selector, pieces, preferred_element_type=jnp.float32)
    return summed.reshape(groups * row_count, width)


def on_device(image, extrapolated, vis_dual, tree_dual, observed, kernel, block_index, live_blocks):
    precise = lax.Precision.HIGHEST
    slab_rows, slab_cols = image.shape
    n_vis = lax.axis_size("vis")
    n_tile = lax.axis_size("tile")
    vis_id = lax.axis_index("vis")
    tile_id = lax.axis_index("tile")
    len_rows = slab_rows * n_vis
    len_cols = slab_cols * n_tile
    block_width = kernel.shape[0]
    chunk = slab_cols // n_vis
    slot_count = vis_dual.shape[0]
    norm_scale = 1.0 / math.sqrt(len_rows * len_cols)
    columns = lax.all_to_all(extrapolated, "vis", split_axis=1, concat_axis=0, tiled=True)
    spec_real, spec_imag = transform_axis(columns, None, -1.0, 0, False)
    all_index = lax.all_gather(block_index.astype(jnp.float32), ("vis", "tile"), tiled=True)
    all_index = all_index.astype(jnp.int32)
    total_blocks = all_index.shape[0]
    owner = jnp.arange(total_blocks, dtype=jnp.int32) // slot_count
    per_row = slab_cols // block_width
    local_row = all_index // per_row
    row_of = (owner // n_tile) * slab_rows + local_row
    band_of = (owner % n_tile) * per_row + all_index % per_row
    col_ids = tile_id * slab_cols + vis_id * chunk + jnp.arange(chunk, dtype=jnp.int32)
    band_count = len_cols // block_width
    band_turns = (
        (jnp.arange(band_count, dtype=jnp.int32) * block_width)[:, None] * col_ids[None, :]
    ) % len_cols
    band_angles = band_turns.astype(jnp.float32) * (TWO_PI / len_cols)
    band_both = pick_rows(band_of, jnp.concatenate([jnp.cos(band_angles), jnp.sin(band_angles)], 1))
    band_cos = band_both[:, :chunk]
    band_sin = band_both[:, chunk:]
    cell_turns = (col_ids[:, None] * jnp.arange(block_width, dtype=jnp.int32)[None, :]) % len_cols
    cell_angles = cell_turns.astype(jnp.float32) * (TWO_PI / len_cols)
    cell_cos = jnp.cos(cell_angles)
    cell_sin = jnp.sin(cell_angles)
    picked = jnp.take(jnp.concatenate([spec_real, spec_imag], axis=1), row_of, axis=0)
    picked_real = picked[:, :chunk]
    picked_imag = picked[:, chunk:]
    twisted_real = picked_real * band_cos + picked_imag * band_sin
    twisted_imag = picked_imag * band_cos - picked_real * band_sin
    group_size = total_blocks // n_vis
    halves = []
    for half in range(2):
        lo = half * (group_size // 2)
        hi = lo + group_size // 2
        half_real = twisted_real.reshape(n_vis, group_size, chunk)[:, lo:hi].reshape(-1, chunk)
        half_imag = twisted_imag.reshape(n_vis, group_size, chunk)[:, lo:hi].reshape(-1, chunk)
        part_real = jnp.dot(half_real, cell_cos, precision=precise) + jnp.dot(
            half_imag, cell_sin, precision=precise
        )
        part_imag = jnp.dot(half_imag, cell_cos, precision=precise) - jnp.dot(
            half_real, cell_sin, precision=precise
        )
        partial = jnp.stack([part_real, part_imag], axis=1)
        halves.append(lax.psum_scatter(partial, "vis", scatter_dimension=0, tiled=True))
    partial = jnp.concatenate(halves, axis=0)
    chosen = lax.psum_scatter(partial, "tile", scatter_dimension=0, tiled=True) * norm_scale
    model = jnp.einsum("ij,csj->csi", kernel, chosen, precision=precise)
    live_mask = (jnp.arange(slot_count, dtype=jnp.int32) < live_blocks[0]).astype(jnp.float32)[
        :, None, None
    ]
    misfit = (vis_dual / 0.5 + model - observed) * live_mask
    totals = lax.psum((jnp.sum(misfit * misfit), jnp.sum(live_mask)), ("vis", "tile"))
    radius = jnp.sqrt(2.0 * block_width * totals[1])
    size_now = jnp.sqrt(totals[0])
    vis_next = 0.5 * misfit * (1.0 - radius / jnp.maximum(size_now, radius))
    contrib = jnp.einsum("ij,csi->csj", kernel, vis_next, precision=precise)
    every = lax.all_gather(contrib, "tile", tiled=True)
    every = lax.all_gather(every, "vis", tiled=True)
    back_real = jnp.dot(every[:, 0, :], cell_cos.T, precision=precise) - jnp.dot(
        every[:, 1, :], cell_sin.T, precision=precise
    )
    back_imag = jnp.dot(every[:, 0, :], cell_sin.T, precision=precise) + jnp.dot(
        every[:, 1, :], cell_cos.T, precision=precise
    )
    turned_real = back_real * band_cos - back_imag * band_sin
    turned_imag = back_real * band_sin + back_imag * band_cos
    turned = jnp.concatenate([turned_real, turned_imag], axis=1)
    turned = turned.reshape(n_vis, total_blocks // n_vis, 2 * chunk)
    gridded = rows_to_grid(local_row.reshape(n_vis, total_blocks // n_vis), turned, slab_rows)
    pixel_real, unused_part = transform_axis(gridded[:, :chunk], gridded[:, chunk:], 1.0, 0, True)
    data_term = (
        lax.all_to_all(pixel_real, "vis", split_axis=0, concat_axis=1, tiled=True) * norm_scale
    )
    approx_one, detail_one = analyse_local(extrapolated)
    approx_two, detail_two = analyse_local(approx_one)
    child = tree_dual[0] + 0.5 * detail_one
    parent = tree_dual[1] + 0.5 * jnp.repeat(detail_two, 2, axis=1)
    factor = 1.0 / jnp.maximum(jnp.sqrt(child * child + parent * parent), 1.0)
    child_next = child * factor
    parent_next = parent * factor
    parent_sum = parent_next[:, 0::2] + parent_next[:, 1::2]
    parent_tail = shifted(parent_sum[:, -3:], "tile", 1)
    level_one = upsample(None, jnp.concatenate([parent_tail, parent_sum], axis=1))
    both_tails = shifted(jnp.stack([level_one[:, -3:], child_next[:, -3:]]), "tile", 1)
    prior_term = upsample(
        jnp.concatenate([both_tails[0], level_one], axis=1),
        jnp.concatenate([both_tails[1], child_next], axis=1),
    )
    image_next = jnp.maximum(image - 0.5 * (data_term + prior_term), 0.0)
    return (image_next, vis_next, jnp.stack([child_next, parent_next]))


def solution(mesh):
    return jax.shard_map(
        on_device,
        mesh=mesh,
        in_specs=(
            P("vis", "tile"),
            P("vis", "tile"),
            P(("vis", "tile"), None, None),
            P(None, "vis", "tile"),
            P(("vis", "tile"), None, None),
            P(),
            P(("vis", "tile")),
            P(("vis", "tile")),
        ),
        out_specs=(P("vis", "tile"), P(("vis", "tile"), None, None), P(None, "vis", "tile")),
        check_vma=False,
    )
```

```python
import math

import jax
import jax.numpy as jnp
from jax import lax
from jax.sharding import PartitionSpec as P

LOW_TAPS = (
    -0.010597401784997278,
    0.032883011666982945,
    0.030841381835986965,
    -0.18703481171888114,
    -0.02798376941698385,
    0.6308807679295904,
    0.7148465705525415,
    0.23037781330885523,
)
HIGH_TAPS = tuple(
    ((1.0 if position % 2 == 0 else -1.0) * LOW_TAPS[7 - position] for position in range(8))
)
TWO_PI = 2.0 * math.pi


def shifted(block, axis, distance):
    devices = range(lax.axis_size(axis))
    route = [((i - distance) % len(devices), i) for i in devices]
    return lax.ppermute(block, axis, route)


def phase_table(left_ids, right_ids, period):
    turns = left_ids[:, None] * right_ids[None, :] % period
    angles = turns.astype(jnp.float32) * (TWO_PI / period)
    return (jnp.cos(angles), jnp.sin(angles))


def factor_pair(length):
    chosen_factor = 1
    for candidate in range(1, math.isqrt(length) + 1):
        if length % candidate == 0:
            chosen_factor = candidate
    return (chosen_factor, length // chosen_factor)


def complex_einsum(form, left_real, left_imag, table_cos, table_sin, real_only):
    precise = lax.Precision.HIGHEST
    real_part = jnp.einsum(form, left_real, table_cos, precision=precise)
    if left_imag is not None:
        real_part = real_part - jnp.einsum(form, left_imag, table_sin, precision=precise)
    if real_only:
        return (real_part, None)
    imag_part = jnp.einsum(form, left_real, table_sin, precision=precise)
    if left_imag is not None:
        imag_part = imag_part + jnp.einsum(form, left_imag, table_cos, precision=precise)
    return (imag_part * 0.0 + real_part, imag_part)


def transform_axis(real_in, imag_in, sign_value, along, real_only):
    length = real_in.shape[along]
    first_factor, second_factor = factor_pair(length)
    first_ids = jnp.arange(first_factor, dtype=jnp.int32)
    second_ids = jnp.arange(second_factor, dtype=jnp.int32)
    cos_first, sin_first = phase_table(first_ids, first_ids, first_factor)
    cos_twist, sin_twist = phase_table(first_ids, second_ids, length)
    cos_second, sin_second = phase_table(second_ids, second_ids, second_factor)
    sin_twist = sign_value * sin_twist
    if along == 0:
        other_len = real_in.shape[1]
        shape_in = (first_factor, second_factor, other_len)
        form_first = "abm,ca->cbm"
        form_second = "cbm,db->dcm"
        cos_twist = cos_twist[:, :, None]
        sin_twist = sin_twist[:, :, None]
        shape_out = (length, other_len)
    else:
        other_len = real_in.shape[0]
        shape_in = (other_len, first_factor, second_factor)
        form_first = "mab,ca->mcb"
        form_second = "mcb,db->mdc"
        cos_twist = cos_twist[None, :, :]
        sin_twist = sin_twist[None, :, :]
        shape_out = (other_len, length)
    shaped_real = real_in.reshape(shape_in)
    shaped_imag = None if imag_in is None else imag_in.reshape(shape_in)
    section_real, section_imag = complex_einsum(
        form_first, shaped_real, shaped_imag, cos_first, sign_value * sin_first, False
    )
    twisted_real = section_real * cos_twist - section_imag * sin_twist
    twisted_imag = section_real * sin_twist + section_imag * cos_twist
    out_real, out_imag = complex_einsum(
        form_second, twisted_real, twisted_imag, cos_second, sign_value * sin_second, real_only
    )
    if real_only:
        return (out_real.reshape(shape_out), None)
    return (out_real.reshape(shape_out), out_imag.reshape(shape_out))


def analyse_local(coarse):
    half_rows = coarse.shape[1] // 2
    next_rows = shifted(coarse[:, :6], "tile", -1)
    extended = jnp.concatenate([coarse, next_rows], axis=1)
    phases = [
        lax.slice_in_dim(extended, parity, extended.shape[1], 2, 1) for parity in range(2)
    ]
    approx = jnp.zeros((coarse.shape[0], half_rows), jnp.float32)
    detail = jnp.zeros_like(approx)
    for position in range(8):
        strided = lax.slice_in_dim(phases[position % 2], position // 2, position // 2 + half_rows, 1, 1)
        approx = approx + LOW_TAPS[position] * strided
        detail = detail + HIGH_TAPS[position] * strided
    return (approx, detail)


def upsample(ext_approx, ext_detail):
    out_rows = ext_detail.shape[1] - 3
    even_part = jnp.zeros((ext_detail.shape[0], out_rows), jnp.float32)
    odd_part = jnp.zeros_like(even_part)
    for lag_index in range(4):
        window_detail = ext_detail[:, 3 - lag_index : 3 - lag_index + out_rows]
        even_part = even_part + HIGH_TAPS[2 * lag_index] * window_detail
        odd_part = odd_part + HIGH_TAPS[2 * lag_index + 1] * window_detail
        if ext_approx is not None:
            window_approx = ext_approx[:, 3 - lag_index : 3 - lag_index + out_rows]
            even_part = even_part + LOW_TAPS[2 * lag_index] * window_approx
            odd_part = odd_part + LOW_TAPS[2 * lag_index + 1] * window_approx
    return jnp.stack([even_part, odd_part], axis=2).reshape(ext_detail.shape[0], 2 * out_rows)


def split_three(values, axis):
    first = lax.reduce_precision(values, exponent_bits=8, mantissa_bits=7)
    rest = values - first
    second = lax.reduce_precision(rest, exponent_bits=8, mantissa_bits=7)
    third = rest - second
    pieces = [first, second, third]
    return jnp.concatenate([piece.astype(jnp.bfloat16) for piece in pieces], axis=axis)


def pick_rows(index, table):
    selector = (index[:, None] == jnp.arange(table.shape[0], dtype=jnp.int32)[None, :]).astype(
        jnp.bfloat16
    )
    selector = jnp.concatenate([selector] * 3, axis=1)
    return jnp.dot(selector, split_three(table, 0), preferred_element_type=jnp.float32)


def rows_to_grid(local_rows, values, row_count):
    groups, members, width = values.shape
    pieces = split_three(values, 1)
    selector = (
        jnp.arange(row_count, dtype=jnp.int32)[None, :, None] == local_rows[:, None, :]
    ).astype(jnp.bfloat16)
    selector = jnp.concatenate([selector] * 3, axis=2)
    summed = jnp.einsum("gkb,gbc->gkc", selector, pieces, preferred_element_type=jnp.float32)
    return summed.reshape(groups * row_count, width)


def on_device(image, extrapolated, vis_dual, tree_dual, observed, kernel, block_index, live_blocks):
    precise = lax.Precision.HIGHEST
    slab_rows, slab_cols = image.shape
    n_vis = lax.axis_size("vis")
    n_tile = lax.axis_size("tile")
    vis_id = lax.axis_index("vis")
    tile_id = lax.axis_index("tile")
    len_rows = slab_rows * n_vis
    len_cols = slab_cols * n_tile
    block_width = kernel.shape[0]
    chunk = slab_cols // n_vis
    slot_count = vis_dual.shape[0]
    norm_scale = 1.0 / math.sqrt(len_rows * len_cols)
    columns = lax.all_to_all(extrapolated, "vis", split_axis=1, concat_axis=0, tiled=True)
    spec_real, spec_imag = transform_axis(columns, None, -1.0, 0, False)
    all_index = lax.all_gather(block_index.astype(jnp.float32), ("vis", "tile"), tiled=True)
    all_index = all_index.astype(jnp.int32)
    total_blocks = all_index.shape[0]
    owner = jnp.arange(total_blocks, dtype=jnp.int32) // slot_count
    per_row = slab_cols // block_width
    local_row = all_index // per_row
    row_of = (owner // n_tile) * slab_rows + local_row
    band_of = (owner % n_tile) * per_row + all_index % per_row
    col_ids = tile_id * slab_cols + vis_id * chunk + jnp.arange(chunk, dtype=jnp.int32)
    band_count = len_cols // block_width
    band_turns = (
        (jnp.arange(band_count, dtype=jnp.int32) * block_width)[:, None] * col_ids[None, :]
    ) % len_cols
    band_angles = band_turns.astype(jnp.float32) * (TWO_PI / len_cols)
    band_both = pick_rows(band_of, jnp.concatenate([jnp.cos(band_angles), jnp.sin(band_angles)], 1))
    band_cos = band_both[:, :chunk]
    band_sin = band_both[:, chunk:]
    cell_turns = (col_ids[:, None] * jnp.arange(block_width, dtype=jnp.int32)[None, :]) % len_cols
    cell_angles = cell_turns.astype(jnp.float32) * (TWO_PI / len_cols)
    cell_cos = jnp.cos(cell_angles)
    cell_sin = jnp.sin(cell_angles)
    picked = jnp.take(jnp.concatenate([spec_real, spec_imag], axis=1), row_of, axis=0)
    picked_real = picked[:, :chunk]
    picked_imag = picked[:, chunk:]
    twisted_real = picked_real * band_cos + picked_imag * band_sin
    twisted_imag = picked_imag * band_cos - picked_real * band_sin
    group_size = total_blocks // n_vis
    halves = []
    pieces_count = 4
    for half in range(pieces_count):
        lo = half * (group_size // pieces_count)
        hi = lo + group_size // pieces_count
        half_real = twisted_real.reshape(n_vis, group_size, chunk)[:, lo:hi].reshape(-1, chunk)
        half_imag = twisted_imag.reshape(n_vis, group_size, chunk)[:, lo:hi].reshape(-1, chunk)
        part_real = jnp.dot(half_real, cell_cos, precision=precise) + jnp.dot(
            half_imag, cell_sin, precision=precise
        )
        part_imag = jnp.dot(half_imag, cell_cos, precision=precise) - jnp.dot(
            half_real, cell_sin, precision=precise
        )
        partial = jnp.stack([part_real, part_imag], axis=1)
        halves.append(lax.psum_scatter(partial, "vis", scatter_dimension=0, tiled=True))
    partial = jnp.concatenate(halves, axis=0)
    chosen = lax.psum_scatter(partial, "tile", scatter_dimension=0, tiled=True) * norm_scale
    model = jnp.einsum("ij,csj->csi", kernel, chosen, precision=precise)
    live_mask = (jnp.arange(slot_count, dtype=jnp.int32) < live_blocks[0]).astype(jnp.float32)[
        :, None, None
    ]
    misfit = (vis_dual / 0.5 + model - observed) * live_mask
    totals = lax.psum((jnp.sum(misfit * misfit), jnp.sum(live_mask)), ("vis", "tile"))
    radius = jnp.sqrt(2.0 * block_width * totals[1])
    size_now = jnp.sqrt(totals[0])
    vis_next = 0.5 * misfit * (1.0 - radius / jnp.maximum(size_now, radius))
    contrib = jnp.einsum("ij,csi->csj", kernel, vis_next, precision=precise)
    every = lax.all_gather(contrib, "tile", tiled=True)
    every = lax.all_gather(every, "vis", tiled=True)
    back_real = jnp.dot(every[:, 0, :], cell_cos.T, precision=precise) - jnp.dot(
        every[:, 1, :], cell_sin.T, precision=precise
    )
    back_imag = jnp.dot(every[:, 0, :], cell_sin.T, precision=precise) + jnp.dot(
        every[:, 1, :], cell_cos.T, precision=precise
    )
    turned_real = back_real * band_cos - back_imag * band_sin
    turned_imag = back_real * band_sin + back_imag * band_cos
    turned = jnp.concatenate([turned_real, turned_imag], axis=1)
    turned = turned.reshape(n_vis, total_blocks // n_vis, 2 * chunk)
    gridded = rows_to_grid(local_row.reshape(n_vis, total_blocks // n_vis), turned, slab_rows)
    pixel_real, unused_part = transform_axis(gridded[:, :chunk], gridded[:, chunk:], 1.0, 0, True)
    data_term = (
        lax.all_to_all(pixel_real, "vis", split_axis=0, concat_axis=1, tiled=True) * norm_scale
    )
    approx_one, detail_one = analyse_local(extrapolated)
    approx_two, detail_two = analyse_local(approx_one)
    child = tree_dual[0] + 0.5 * detail_one
    parent = tree_dual[1] + 0.5 * jnp.repeat(detail_two, 2, axis=1)
    factor = 1.0 / jnp.maximum(jnp.sqrt(child * child + parent * parent), 1.0)
    child_next = child * factor
    parent_next = parent * factor
    parent_sum = parent_next[:, 0::2] + parent_next[:, 1::2]
    parent_tail = shifted(parent_sum[:, -3:], "tile", 1)
    level_one = upsample(None, jnp.concatenate([parent_tail, parent_sum], axis=1))
    both_tails = shifted(jnp.stack([level_one[:, -3:], child_next[:, -3:]]), "tile", 1)
    prior_term = upsample(
        jnp.concatenate([both_tails[0], level_one], axis=1),
        jnp.concatenate([both_tails[1], child_next], axis=1),
    )
    image_next = jnp.maximum(image - 0.5 * (data_term + prior_term), 0.0)
    return (image_next, vis_next, jnp.stack([child_next, parent_next]))


def solution(mesh):
    return jax.shard_map(
        on_device,
        mesh=mesh,
        in_specs=(
            P("vis", "tile"),
            P("vis", "tile"),
            P(("vis", "tile"), None, None),
            P(None, "vis", "tile"),
            P(("vis", "tile"), None, None),
            P(),
            P(("vis", "tile")),
            P(("vis", "tile")),
        ),
        out_specs=(P("vis", "tile"), P(("vis", "tile"), None, None), P(None, "vis", "tile")),
        check_vma=False,
    )
```
